32 devices in a mesh: groups: 2 (over y), seq: 4 (over z), head: 2 (over x), rep: 2 (over core).
Axes of the slice: x: 2, y: 2, z: 4, core: 2. Of those that a mesh axis runs over, the one named last changes fastest.
Arguments:
- segment_ids: int32 [2048], P(('groups', 'seq')), parts along dimension 0, may hold values from 0 to 3, never falling along the last dimension, each value on 1 to 640 neighbouring positions
- window_query: bfloat16 [2048, 8, 512], P(('groups', 'seq'), 'head', 'rep'), parts along dimension 0, may hold values from -120 to 120
- window_keys: bfloat16 [2048, 512], P(('groups', 'seq'), 'head'), parts along dimension 0, may hold values from -4 to 4
- window_values: bfloat16 [2048, 512], P(('groups', 'seq'), 'head'), parts along dimension 0, may hold values from -6 to 6
- window_grad_out: bfloat16 [2048, 8, 512], P(('groups', 'seq'), 'head', 'rep'), parts along dimension 0, may hold values from -6 to 6
- window_sinks: float32 [8, 8], P('head', 'rep'), may hold values from 1 to 6
- full_query: bfloat16 [2048, 8, 512], P(('groups', 'seq'), 'head', 'rep'), parts along dimension 0, may hold values from -120 to 120
- full_keys: bfloat16 [2048, 512], P(('groups', 'seq'), 'head'), parts along dimension 0, may hold values from -4 to 4
- full_values: bfloat16 [2048, 512], P(('groups', 'seq'), 'head'), parts along dimension 0, may hold values from -6 to 6
- full_grad_out: bfloat16 [2048, 8, 512], P(('groups', 'seq'), 'head', 'rep'), parts along dimension 0, may hold values from -6 to 6
- full_sinks: float32 [8, 8], P('head', 'rep'), may hold values from 1 to 6
Outputs:
- window_dq: bfloat16 [2048, 8, 512], P(('groups', 'seq'), 'head', 'rep'), parts along dimension 0
- window_dk: bfloat16 [2048, 512], P(('groups', 'seq'), 'head'), parts along dimension 0
- window_dv: bfloat16 [2048, 512], P(('groups', 'seq'), 'head'), parts along dimension 0
- full_dq: bfloat16 [2048, 8, 512], P(('groups', 'seq'), 'head', 'rep'), parts along dimension 0
- full_dk: bfloat16 [2048, 512], P(('groups', 'seq'), 'head'), parts along dimension 0
- full_dv: bfloat16 [2048, 512], P(('groups', 'seq'), 'head'), parts along dimension 0
The draws below stay inside these ranges and needn't reach their ends.
There are 2 independent parts, one for each index of `groups`. The reference program is written for one: setup_inputs(seed, part) draws one part's arguments, and reference() takes and returns one part's arrays. A program takes and returns all parts, laid end to end along the dimension named above; an argument that names none is the same for every part. Nothing has to cross between parts.
Inputs may be any that keep to these rules, and one draw needn't show every extreme that they name: `segment_ids`: ids never fall along the sequence; there are 4 documents, the longest exactly 640 positions.
All inputs are finite; a program needn't handle non-finite values.
Results may differ from the reference program's by a relative error of at most 0.02.
Values may be sent and summed in bfloat16 or wider, within the bound.
No kernel may reach another device: no remote copies, remote signals or barrier semaphores. Data moves between devices by JAX's collectives and lax.ppermute only.
A program may use at most 64 MiB of HBM per device.

```python
import math
from functools import partial
import jax
import jax.numpy as jnp
import numpy as np
from jax import lax

KVH = 8
QPK = 8
HD = 64
WINDOW = 128
DOCS = 4
TOKENS = 1024
LONGEST = 640


def shared_keys(key, salt):
    base = jax.random.normal(jax.random.fold_in(key, salt), (TOKENS, KVH, HD), jnp.float32)
    base = jnp.clip(base, -4.0, 4.0)
    return base


def query_draw(key, salt):
    noise = jax.random.normal(jax.random.fold_in(key, salt), (TOKENS, KVH, QPK, HD), jnp.float32)
    noise = jnp.clip(noise, -4.0, 4.0)
    return noise.reshape(TOKENS, KVH, QPK * HD).astype(jnp.bfloat16)


def draw_window_query(key, part):
    return query_draw(key, 21)


def draw_window_keys(key, part):
    return shared_keys(key, 22).reshape(TOKENS, KVH * HD).astype(jnp.bfloat16)


def draw_full_query(key, part):
    return query_draw(key, 31)


def draw_full_keys(key, part):
    return shared_keys(key, 32).reshape(TOKENS, KVH * HD).astype(jnp.bfloat16)


def level_of(own_key, dims, shards, low, top_value):
    def one(axis_at, shards_of):
        steps = jax.random.uniform(jax.random.fold_in(jax.random.fold_in(own_key, 6), axis_at), (shards_of,), jnp.float32, low / len(shards), top_value / len(shards))
        return jnp.repeat(jnp.exp(steps), dims[axis_at] // shards_of).reshape((-1,) + (1,) * (len(dims) - axis_at - 1))

    loudness = one(*shards[0])
    for cut in shards[1:]:
        loudness = loudness * one(*cut)
    return loudness


def profile(amount, total, most, skew):
    portions = [(1 << 20) // math.isqrt(grade ** skew) + 1 for grade in range(2, amount + 1)]
    surplus, given = total - most - (amount - 1), [1] * (amount - 1)
    while surplus > 0:
        candidates = [i for i in range(amount - 1) if given[i] < most]
        whole, remaining = sum([portions[i] for i in candidates]), surplus
        for i in candidates:
            more = min(most - given[i], max(1, remaining * portions[i] // whole), surplus)
            given[i] = given[i] + more
            surplus = surplus - more
    return np.array([most] + given)


def ragged_sizes(key, number_of, total, reach, slope):
    if number_of == 2:
        one = jax.random.randint(key, (), max(1, total - reach), min(reach, total - 1) + 1)
        return jnp.stack([one, total - one])
    lengths = jnp.asarray(profile(number_of, total, reach, slope), jnp.int32)
    couples = (number_of - 1) // 2
    donor, sink = lengths[1:1 + 2 * couples:2], lengths[2:2 + 2 * couples:2]
    margin = jnp.minimum(donor - 1, reach - sink)
    moved = jax.random.randint(jax.random.fold_in(key, 1), (couples,), 0, 1 << 20) % (margin + 1)
    lengths = lengths.at[1:1 + 2 * couples:2].set(donor - moved).at[2:2 + 2 * couples:2].set(sink + moved)
    return lengths[jax.random.permutation(jax.random.fold_in(key, 2), number_of)]


def scatter_about(own_key, extent, deviation, limit, shards=(), kind=jnp.bfloat16):
    entries = deviation * jax.random.normal(own_key, extent, jnp.float32)
    if shards:
        entries = entries * level_of(own_key, extent, shards, -0.22, 0.18)
    return jnp.clip(entries, -limit, limit).astype(kind)


def setup_inputs(seed: int = 0, part: int = 0) -> dict:
    seeds = jax.random.split(jax.random.key(seed), 12)
    own_keys = jax.random.split(jax.random.fold_in(seeds[11], part), 12)
    segment_ids = jnp.searchsorted(jnp.cumsum(ragged_sizes(own_keys[0], DOCS, TOKENS, LONGEST, 2)), jnp.arange(TOKENS), side="right").astype(jnp.int32)
    window_query = draw_window_query(jax.random.fold_in(jax.random.fold_in(seeds[11], part), 71), part)
    window_keys = draw_window_keys(jax.random.fold_in(jax.random.fold_in(seeds[11], part), 71), part)
    window_values = scatter_about(own_keys[3], (TOKENS, KVH * HD), 1.0, 6.0, ((0, 4), (1, 2)))
    window_grad_out = scatter_about(own_keys[4], (TOKENS, KVH, QPK * HD), 1.0, 6.0, ((0, 4), (1, 2), (2, 2)))
    window_sinks = jnp.clip(1.0 + 5.0 * jax.random.uniform(seeds[5], (KVH, QPK), jnp.float32) ** level_of(seeds[5], (KVH, QPK), ((0, 2), (1, 2)), -0.2, 0.2), 1.0, 6.0)
    full_query = draw_full_query(jax.random.fold_in(jax.random.fold_in(seeds[11], part), 71), part)
    full_keys = draw_full_keys(jax.random.fold_in(jax.random.fold_in(seeds[11], part), 71), part)
    full_values = scatter_about(own_keys[8], (TOKENS, KVH * HD), 1.0, 6.0, ((0, 4), (1, 2)))
    full_grad_out = scatter_about(own_keys[9], (TOKENS, KVH, QPK * HD), 1.0, 6.0, ((0, 4), (1, 2), (2, 2)))
    full_sinks = jnp.clip(1.0 + 5.0 * jax.random.uniform(seeds[10], (KVH, QPK), jnp.float32) ** level_of(seeds[10], (KVH, QPK), ((0, 2), (1, 2)), -0.2, 0.2), 1.0, 6.0)
    return {"segment_ids": segment_ids, "window_query": window_query, "window_keys": window_keys, "window_values": window_values, "window_grad_out": window_grad_out, "window_sinks": window_sinks, "full_query": full_query, "full_keys": full_keys, "full_values": full_values, "full_grad_out": full_grad_out, "full_sinks": full_sinks}


neg_big = -1e+30

def softmax_grads(scores, visible, sink_logit, value_rows, grad_rows, query_rows, key_rows, score_scale):
    wide = jnp.float32
    masked = jnp.where(visible, scores, neg_big)
    row_max = jnp.maximum(lax.optimization_barrier(jnp.max(masked, axis=-1)), sink_logit)
    denominator = lax.optimization_barrier(jnp.sum(jnp.exp(masked - row_max[..., None]), axis=-1)) + jnp.exp(sink_logit - row_max)
    log_total = row_max + jnp.log(denominator)
    weights = jnp.where(visible, jnp.exp(masked - log_total[..., None]), 0.0)
    weights_low = lax.optimization_barrier(weights.astype(jnp.bfloat16)).astype(wide)
    values_wide = value_rows.astype(wide)
    grads_wide = grad_rows.astype(wide)
    attended = jnp.einsum('...qk,...kd->...qd', weights_low, values_wide)
    row_delta = lax.optimization_barrier(jnp.sum(grads_wide * attended, axis=-1))
    grad_weights = jnp.einsum('...qd,...kd->...qk', grads_wide, values_wide)
    grad_scores = weights * (grad_weights - row_delta[..., None])
    scores_low = lax.optimization_barrier(grad_scores.astype(jnp.bfloat16)).astype(wide)
    query_grad = jnp.einsum('...qk,...kd->...qd', scores_low, key_rows.astype(wide)) * score_scale
    key_grad = jnp.einsum('...qk,...qd->...kd', scores_low, query_rows.astype(wide)) * score_scale
    value_grad = jnp.einsum('...qk,...qd->...kd', weights_low, grads_wide)
    return (query_grad, key_grad, value_grad)

def query_heads(array):
    return jnp.transpose(array.reshape(TOKENS, KVH, QPK, HD), (1, 2, 0, 3)).reshape(KVH * QPK, TOKENS, HD)

def key_heads(array):
    return jnp.transpose(array.reshape(TOKENS, KVH, HD), (1, 0, 2))

def pack_queries(grads):
    return jnp.transpose(grads.reshape(KVH, QPK, TOKENS, HD), (2, 0, 1, 3)).reshape(TOKENS, KVH, QPK * HD).astype(jnp.bfloat16)

def pack_keys(grads):
    summed = grads.reshape(KVH, QPK, TOKENS, HD).sum(axis=1)
    return jnp.transpose(summed, (1, 0, 2)).reshape(TOKENS, KVH * HD).astype(jnp.bfloat16)

def band(array, fill):
    nblocks = TOKENS // WINDOW
    padded = jnp.concatenate([jnp.full((WINDOW,) + array.shape[1:], fill, array.dtype), array], axis=0)
    blocks = padded.reshape((nblocks + 1, WINDOW) + array.shape[1:])
    return jnp.concatenate([blocks[:-1], blocks[1:]], axis=1)

def unband(grads):
    later = jnp.concatenate([grads[1:, :WINDOW], jnp.zeros_like(grads[:1, :WINDOW])], axis=0)
    return (grads[:, WINDOW:] + later).reshape(TOKENS, HD)

def full_head(head_item, key_all, value_all, visible, score_scale):
    query_h, grad_h, sink_logit, group = head_item
    key_h = lax.dynamic_index_in_dim(key_all, group, 0, keepdims=False)
    value_h = lax.dynamic_index_in_dim(value_all, group, 0, keepdims=False)
    scores = jnp.dot(query_h, key_h.T, preferred_element_type=jnp.float32) * score_scale
    return softmax_grads(scores, visible, sink_logit, value_h, grad_h, query_h, key_h, score_scale)

def window_head(head_item, key_all, value_all, visible, score_scale):
    query_h, grad_h, sink_logit, group = head_item
    nblocks = TOKENS // WINDOW
    key_h = band(lax.dynamic_index_in_dim(key_all, group, 0, keepdims=False), 0.0)
    value_h = band(lax.dynamic_index_in_dim(value_all, group, 0, keepdims=False), 0.0)
    query_b = query_h.reshape(nblocks, WINDOW, HD)
    grad_b = grad_h.reshape(nblocks, WINDOW, HD)
    scores = jnp.einsum('nqd,nkd->nqk', query_b.astype(jnp.float32), key_h.astype(jnp.float32)) * score_scale
    query_grad, key_grad, value_grad = softmax_grads(scores, visible, sink_logit, value_h, grad_b, query_b, key_h, score_scale)
    return (query_grad.reshape(TOKENS, HD), unband(key_grad), unband(value_grad))

def run_layer(head_fn, visible, query_rows, key_rows, value_rows, grad_rows, sink_logits):
    score_scale = 1.0 / math.sqrt(HD)
    group_ids = (jnp.arange(KVH * QPK, dtype=jnp.int32) // QPK).astype(jnp.int32)
    items = (query_heads(query_rows), query_heads(grad_rows), sink_logits.reshape(KVH * QPK), group_ids)
    worker = partial(head_fn, key_all=key_heads(key_rows), value_all=key_heads(value_rows), visible=visible, score_scale=score_scale)
    query_grad, key_grad, value_grad = lax.map(worker, items)
    return (pack_queries(query_grad), pack_keys(key_grad), pack_keys(value_grad))

def reference(segment_ids, window_query, window_keys, window_values, window_grad_out, window_sinks, full_query, full_keys, full_values, full_grad_out, full_sinks):
    nblocks = TOKENS // WINDOW
    positions = jnp.arange(TOKENS, dtype=jnp.int32)
    query_pos = positions.reshape(nblocks, WINDOW)
    key_pos = band(positions, -4 * TOKENS)
    query_seg = segment_ids.reshape(nblocks, WINDOW)
    key_seg = band(segment_ids, -1)
    distance = query_pos[:, :, None] - key_pos[:, None, :]
    window_visible = (distance >= 0) & (distance < WINDOW) & (query_seg[:, :, None] == key_seg[:, None, :])
    window_dq, window_dk, window_dv = run_layer(window_head, window_visible, window_query, window_keys, window_values, window_grad_out, window_sinks)
    full_visible = (positions[:, None] >= positions[None, :]) & (segment_ids[:, None] == segment_ids[None, :])
    full_dq, full_dk, full_dv = run_layer(full_head, full_visible, full_query, full_keys, full_values, full_grad_out, full_sinks)
    return (window_dq, window_dk, window_dv, full_dq, full_dk, full_dv)
```

```python
import functools
import math

import jax
import jax.numpy as jnp
from jax import lax
from jax.experimental import pallas as pl
from jax.experimental.pallas import tpu as pltpu
from jax.sharding import PartitionSpec as P

HD = 64
WINDOW = 128
NEG = -1e30
NT_DIMS = (((1,), (1,)), ((), ()))


def passed_along(value, axis, steps):
    count = lax.axis_size(axis)
    first, last = (max(0, -steps), min(count, count - steps))
    return lax.ppermute(value, axis, [(source, source + steps) for source in range(first, last)])


def pick_half(block, half):
    return jnp.where(half == 0, block[:, :HD], block[:, HD:])


def attn_bwd_kernel(sink_ref, q_ref, do_ref, k_ref, v_ref, bias_ref, dq_ref, dk_ref, dv_ref):
    g = pl.program_id(0)
    i = pl.program_id(1)
    j = pl.program_id(2)
    groups = dk_ref.shape[1] // HD

    @pl.when((g == 0) & (i == 0) & (j == 0))
    def _():
        dk_ref[...] = jnp.zeros_like(dk_ref)
        dv_ref[...] = jnp.zeros_like(dv_ref)

    k = pick_half(k_ref[...], g % 2)
    v = pick_half(v_ref[...], g % 2)
    q = pick_half(q_ref[...], j % 2)
    do = pick_half(do_ref[...], j % 2)
    sink = sink_ref[g, j]

    s = lax.dot_general(q, k, NT_DIMS, preferred_element_type=jnp.float32) + bias_ref[...]
    row_max = jnp.maximum(jnp.max(s, axis=1, keepdims=True), sink)
    e = jnp.exp(s - row_max)
    total = jnp.sum(e, axis=1, keepdims=True) + jnp.exp(sink - row_max)
    p = e * (1.0 / total)
    p_low = p.astype(jnp.bfloat16)
    o = jnp.dot(p_low, v, preferred_element_type=jnp.float32)
    delta = jnp.sum(do.astype(jnp.float32) * o, axis=1, keepdims=True)
    dp = lax.dot_general(do, v, NT_DIMS, preferred_element_type=jnp.float32)
    ds_low = (p * (dp - delta)).astype(jnp.bfloat16)
    dq = (jnp.dot(ds_low, k, preferred_element_type=jnp.float32) * 0.125).astype(dq_ref.dtype)
    dk = jnp.dot(ds_low.T, q, preferred_element_type=jnp.float32)
    dv = jnp.dot(p_low.T, do, preferred_element_type=jnp.float32)

    @pl.when(j % 2 == 0)
    def _():
        dq_ref[:, :HD] = dq

    @pl.when(j % 2 == 1)
    def _():
        dq_ref[:, HD:] = dq

    for gg in range(groups):
        @pl.when(g == gg)
        def _():
            dk_ref[:, gg * HD:(gg + 1) * HD] += dk
            dv_ref[:, gg * HD:(gg + 1) * HD] += dv


def attn_bwd(sinks, queries, grads, keys, values, bias):
    n = queries.shape[0]
    m = keys.shape[0]
    groups, heads = sinks.shape
    rows = n
    while rows > 8 and rows * m > (1 << 18):
        rows //= 2
    grid = (groups, n // rows, heads)

    def q_map(g, i, j):
        return (i, (g * heads + j) // 2)

    return pl.pallas_call(
        attn_bwd_kernel,
        grid=grid,
        in_specs=[
            pl.BlockSpec(memory_space=pltpu.SMEM),
            pl.BlockSpec((rows, 2 * HD), q_map),
            pl.BlockSpec((rows, 2 * HD), q_map),
            pl.BlockSpec((m, 2 * HD), lambda g, i, j: (0, g // 2)),
            pl.BlockSpec((m, 2 * HD), lambda g, i, j: (0, g // 2)),
            pl.BlockSpec((rows, m), lambda g, i, j: (i, 0)),
        ],
        out_specs=[
            pl.BlockSpec((rows, 2 * HD), q_map),
            pl.BlockSpec((m, groups * HD), lambda g, i, j: (0, 0)),
            pl.BlockSpec((m, groups * HD), lambda g, i, j: (0, 0)),
        ],
        out_shape=[
            jax.ShapeDtypeStruct(queries.shape, jnp.bfloat16),
            jax.ShapeDtypeStruct((m, groups * HD), jnp.float32),
            jax.ShapeDtypeStruct((m, groups * HD), jnp.float32),
        ],
        compiler_params=pltpu.CompilerParams(
            dimension_semantics=("arbitrary", "arbitrary", "arbitrary"),
            vmem_limit_bytes=60 * 1024 * 1024,
        ),
    )(sinks, queries, grads, keys, values, bias)


def make_bias(query_pos, query_seg, key_pos, key_seg, window):
    distance = query_pos[:, None] - key_pos[None, :]
    visible = (distance >= 0) & (key_pos[None, :] >= 0) & (query_seg[:, None] == key_seg[None, :])
    if window is not None:
        visible = visible & (distance < window)
    return jnp.where(visible, 0.0, NEG).astype(jnp.float32)


def body(
    segment_ids,
    window_query,
    window_keys,
    window_values,
    window_grad_out,
    window_sinks,
    full_query,
    full_keys,
    full_values,
    full_grad_out,
    full_sinks,
):
    n = window_query.shape[0]
    key_cols = window_keys.shape[1]
    seq_count = lax.axis_size("seq")
    seq_index = lax.axis_index("seq")
    query_pos = seq_index * n + jnp.arange(n)

    full_kv = jnp.concatenate([full_keys, full_values], axis=1)
    received = {}
    for d in range(1, seq_count):
        received[d] = passed_along((full_kv, segment_ids), "seq", d)

    halo_kv, halo_seg = passed_along(
        (
            jnp.concatenate([window_keys[n - WINDOW:], window_values[n - WINDOW:]], axis=1),
            segment_ids[n - WINDOW:],
        ),
        "seq",
        1,
    )
    w_keys = jnp.concatenate([halo_kv[:, :key_cols], window_keys], axis=0)
    w_values = jnp.concatenate([halo_kv[:, key_cols:], window_values], axis=0)
    w_seg = jnp.concatenate([halo_seg, segment_ids], axis=0)
    w_pos = seq_index * n - WINDOW + jnp.arange(n + WINDOW)
    w_bias = make_bias(query_pos, segment_ids, w_pos, w_seg, WINDOW)
    w_q = (window_query.reshape(n, -1) * 0.125).astype(jnp.bfloat16)
    w_do = window_grad_out.reshape(n, -1)
    w_dq, w_dk, w_dv = attn_bwd(window_sinks, w_q, w_do, w_keys, w_values, w_bias)
    back_w = passed_along(
        jnp.concatenate([w_dk[:WINDOW], w_dv[:WINDOW]], axis=1).astype(jnp.bfloat16), "seq", -1
    ).astype(jnp.float32)
    w_kv = jnp.concatenate([w_dk[WINDOW:], w_dv[WINDOW:]], axis=1)
    w_kv = jnp.concatenate([w_kv[: n - WINDOW], w_kv[n - WINDOW:] + back_w], axis=0)

    order = list(range(seq_count - 1, 0, -1))
    f_kv = jnp.concatenate([received[d][0] for d in order] + [full_kv], axis=0)
    f_seg = jnp.concatenate([received[d][1] for d in order] + [segment_ids], axis=0)
    f_pos = (seq_index - (seq_count - 1)) * n + jnp.arange(seq_count * n)
    f_bias = make_bias(query_pos, segment_ids, f_pos, f_seg, None)
    f_q = (full_query.reshape(n, -1) * 0.125).astype(jnp.bfloat16)
    f_do = full_grad_out.reshape(n, -1)
    f_dq, f_dk, f_dv = attn_bwd(
        full_sinks, f_q, f_do, f_kv[:, :key_cols], f_kv[:, key_cols:], f_bias
    )
    f_part = jnp.concatenate([f_dk, f_dv], axis=1)
    f_own = f_part[(seq_count - 1) * n:]
    for jj, d in enumerate(order):
        piece = f_part[jj * n:(jj + 1) * n].astype(jnp.bfloat16)
        f_own = f_own + passed_along(piece, "seq", -d).astype(jnp.float32)

    both = jnp.concatenate([w_kv, f_own], axis=1)
    if lax.axis_size("rep") == 2:
        both = both + lax.ppermute(both, "rep", [(0, 1), (1, 0)])
    else:
        both = lax.psum(both, "rep")
    both = both.astype(jnp.bfloat16)
    return (
        w_dq.reshape(window_query.shape),
        both[:, :key_cols],
        both[:, key_cols:2 * key_cols],
        f_dq.reshape(full_query.shape),
        both[:, 2 * key_cols:3 * key_cols],
        both[:, 3 * key_cols:],
    )


def solution(mesh):
    placed = (
        P(("groups", "seq")),
        P(("groups", "seq"), "head", "rep"),
        P(("groups", "seq"), "head"),
        P(("groups", "seq"), "head"),
        P(("groups", "seq"), "head", "rep"),
        P("head", "rep"),
        P(("groups", "seq"), "head", "rep"),
        P(("groups", "seq"), "head"),
        P(("groups", "seq"), "head"),
        P(("groups", "seq"), "head", "rep"),
        P("head", "rep"),
    )
    return jax.shard_map(
        body,
        mesh=mesh,
        in_specs=placed,
        out_specs=(
            P(("groups", "seq"), "head", "rep"),
            P(("groups", "seq"), "head"),
            P(("groups", "seq"), "head"),
            P(("groups", "seq"), "head", "rep"),
            P(("groups", "seq"), "head"),
            P(("groups", "seq"), "head"),
        ),
        check_vma=False,
    )
```

```python
import functools
import math

import jax
import jax.numpy as jnp
from jax import lax
from jax.experimental import pallas as pl
from jax.experimental.pallas import tpu as pltpu
from jax.sharding import PartitionSpec as P

HD = 64
WINDOW = 128
NEG = -1e30
NT_DIMS = (((1,), (1,)), ((), ()))


def passed_along(value, axis, steps):
    count = lax.axis_size(axis)
    first, last = (max(0, -steps), min(count, count - steps))
    return lax.ppermute(value, axis, [(source, source + steps) for source in range(first, last)])


def pick_half(block, half):
    return jnp.where(half == 0, block[:, :HD], block[:, HD:])


def attn_bwd_kernel(g0, gn, sink_ref, q_ref, do_ref, k_ref, v_ref, bias_ref, dq_ref, dk_ref, dv_ref):
    g_rel = pl.program_id(0)
    g = g_rel + g0
    i = pl.program_id(1)
    j = pl.program_id(2)

    @pl.when((g_rel == 0) & (i == 0) & (j == 0))
    def _():
        dk_ref[...] = jnp.zeros_like(dk_ref)
        dv_ref[...] = jnp.zeros_like(dv_ref)

    k = pick_half(k_ref[...], g % 2)
    v = pick_half(v_ref[...], g % 2)
    q = pick_half(q_ref[...], j % 2)
    do = pick_half(do_ref[...], j % 2)
    sink = sink_ref[g, j]

    s = lax.dot_general(q, k, NT_DIMS, preferred_element_type=jnp.float32) + bias_ref[...]
    row_max = jnp.maximum(jnp.max(s, axis=1, keepdims=True), sink)
    e = jnp.exp(s - row_max)
    total = jnp.sum(e, axis=1, keepdims=True) + jnp.exp(sink - row_max)
    p = e * (1.0 / total)
    p_low = p.astype(jnp.bfloat16)
    o = jnp.dot(p_low, v, preferred_element_type=jnp.float32)
    delta = jnp.sum(do.astype(jnp.float32) * o, axis=1, keepdims=True)
    dp = lax.dot_general(do, v, NT_DIMS, preferred_element_type=jnp.float32)
    ds_low = (p * (dp - delta)).astype(jnp.bfloat16)
    dq = (jnp.dot(ds_low, k, preferred_element_type=jnp.float32) * 0.125).astype(dq_ref.dtype)
    dk = jnp.dot(ds_low.T, q, preferred_element_type=jnp.float32)
    dv = jnp.dot(p_low.T, do, preferred_element_type=jnp.float32)

    @pl.when(j % 2 == 0)
    def _():
        dq_ref[:, :HD] = dq

    @pl.when(j % 2 == 1)
    def _():
        dq_ref[:, HD:] = dq

    for gg in range(gn):
        @pl.when(g_rel == gg)
        def _():
            dk_ref[:, gg * HD:(gg + 1) * HD] += dk
            dv_ref[:, gg * HD:(gg + 1) * HD] += dv


def attn_bwd(sinks, queries, grads, keys, values, bias, g0, gn):
    n = queries.shape[0]
    m = keys.shape[0]
    heads = sinks.shape[1]
    rows = n
    while rows > 8 and rows * m > (1 << 18):
        rows //= 2
    grid = (gn, n // rows, heads)

    def q_map(g, i, j):
        return (i, ((g + g0) * heads + j) // 2)

    def out_q_map(g, i, j):
        return (i, (g * heads + j) // 2)

    return pl.pallas_call(
        functools.partial(attn_bwd_kernel, g0, gn),
        grid=grid,
        in_specs=[
            pl.BlockSpec(memory_space=pltpu.SMEM),
            pl.BlockSpec((rows, 2 * HD), q_map),
            pl.BlockSpec((rows, 2 * HD), q_map),
            pl.BlockSpec((m, 2 * HD), lambda g, i, j: (0, (g + g0) // 2)),
            pl.BlockSpec((m, 2 * HD), lambda g, i, j: (0, (g + g0) // 2)),
            pl.BlockSpec((rows, m), lambda g, i, j: (i, 0)),
        ],
        out_specs=[
            pl.BlockSpec((rows, 2 * HD), out_q_map),
            pl.BlockSpec((m, gn * HD), lambda g, i, j: (0, 0)),
            pl.BlockSpec((m, gn * HD), lambda g, i, j: (0, 0)),
        ],
        out_shape=[
            jax.ShapeDtypeStruct((n, gn * heads * HD), jnp.bfloat16),
            jax.ShapeDtypeStruct((m, gn * HD), jnp.float32),
            jax.ShapeDtypeStruct((m, gn * HD), jnp.float32),
        ],
        compiler_params=pltpu.CompilerParams(
            dimension_semantics=("arbitrary", "arbitrary", "arbitrary"),
            vmem_limit_bytes=60 * 1024 * 1024,
        ),
        cost_estimate=pl.CostEstimate(
            flops=12 * gn * heads * n * m * HD,
            transcendentals=gn * heads * n * m,
            bytes_accessed=4 * n * m + 4 * n * gn * heads * HD * 3 + 12 * m * gn * HD,
        ),
    )(sinks, queries, grads, keys, values, bias)


def make_bias(query_pos, query_seg, key_pos, key_seg, window):
    distance = query_pos[:, None] - key_pos[None, :]
    visible = (distance >= 0) & (key_pos[None, :] >= 0) & (query_seg[:, None] == key_seg[None, :])
    if window is not None:
        visible = visible & (distance < window)
    return jnp.where(visible, 0.0, NEG).astype(jnp.float32)


def seg_rows(ids, width):
    count = ids.shape[0]
    lines = -(-count // width)
    flat = jnp.zeros((16 * (-(-lines // 16)) * width,), jnp.bfloat16)
    flat = flat.at[:count].set(ids.astype(jnp.bfloat16))
    return flat.reshape(-1, width)


def read_seg(block, count):
    return block.reshape(-1)[:count].astype(jnp.float32).astype(jnp.int32)


def body(
    segment_ids,
    window_query,
    window_keys,
    window_values,
    window_grad_out,
    window_sinks,
    full_query,
    full_keys,
    full_values,
    full_grad_out,
    full_sinks,
):
    n = window_query.shape[0]
    cols = window_keys.shape[1]
    groups = cols // HD
    seq_count = lax.axis_size("seq")
    seq_index = lax.axis_index("seq")
    rep_index = lax.axis_index("rep")
    first = rep_index == 0
    query_pos = seq_index * n + jnp.arange(n)
    order = list(range(seq_count - 1, 0, -1))
    swap = [(0, 1), (1, 0)]

    halo_in = jnp.concatenate(
        [
            jnp.concatenate([window_keys[n - WINDOW:], window_values[n - WINDOW:]], axis=1),
            seg_rows(segment_ids[n - WINDOW:], 2 * cols),
        ],
        axis=0,
    )
    halo = passed_along(halo_in, "seq", 1)

    own_half = jnp.where(first, full_keys, full_values)
    seg_block = seg_rows(segment_ids, cols)
    payload = jnp.concatenate([own_half, seg_block], axis=0)
    halo, payload = lax.optimization_barrier((halo, payload))
    arrived = [passed_along(payload, "seq", d) for d in order]

    w_keys = jnp.concatenate([halo[:WINDOW, :cols], window_keys], axis=0)
    w_values = jnp.concatenate([halo[:WINDOW, cols:], window_values], axis=0)
    w_seg = jnp.concatenate([read_seg(halo[WINDOW:], WINDOW), segment_ids], axis=0)
    w_pos = seq_index * n - WINDOW + jnp.arange(n + WINDOW)
    w_bias = make_bias(query_pos, segment_ids, w_pos, w_seg, WINDOW)
    w_q = (window_query.reshape(n, -1) * 0.125).astype(jnp.bfloat16)
    w_do = window_grad_out.reshape(n, -1)
    g_split = groups // 2 if groups > 1 else groups
    w_out1 = attn_bwd(window_sinks, w_q, w_do, w_keys, w_values, w_bias, 0, g_split)

    w_out1, arrived = lax.optimization_barrier((w_out1, arrived))
    mine = jnp.concatenate(arrived, axis=0)
    other = lax.ppermute(mine, "rep", swap)
    step = n + seg_block.shape[0]
    key_parts, value_parts, seg_parts = [], [], []
    for idx in range(len(order)):
        a = mine[idx * step:(idx + 1) * step]
        b = other[idx * step:(idx + 1) * step]
        key_parts.append(jnp.where(first, a[:n], b[:n]))
        value_parts.append(jnp.where(first, b[:n], a[:n]))
        seg_parts.append(read_seg(a[n:], n))
    f_keys = jnp.concatenate(key_parts + [full_keys], axis=0)
    f_values = jnp.concatenate(value_parts + [full_values], axis=0)
    f_seg = jnp.concatenate(seg_parts + [segment_ids], axis=0)
    f_pos = (seq_index - (seq_count - 1)) * n + jnp.arange(seq_count * n)
    f_bias = make_bias(query_pos, segment_ids, f_pos, f_seg, None)
    f_q = (full_query.reshape(n, -1) * 0.125).astype(jnp.bfloat16)
    f_do = full_grad_out.reshape(n, -1)
    f_dq, f_dk, f_dv = attn_bwd(full_sinks, f_q, f_do, f_keys, f_values, f_bias, 0, groups)

    give = jnp.where(first, f_dv, f_dk)
    keep = jnp.where(first, f_dk, f_dv)
    summed = keep + lax.ppermute(give, "rep", swap)
    f_final = summed[(seq_count - 1) * n:]
    for jj, d in enumerate(order):
        piece = summed[jj * n:(jj + 1) * n].astype(jnp.bfloat16)
        f_final = f_final + passed_along(piece, "seq", -d).astype(jnp.float32)

    if g_split < groups:
        w_out2 = attn_bwd(window_sinks, w_q, w_do, w_keys, w_values, w_bias, g_split, groups - g_split)
        w_dq = jnp.concatenate([w_out1[0], w_out2[0]], axis=1)
        w_dk = jnp.concatenate([w_out1[1], w_out2[1]], axis=1)
        w_dv = jnp.concatenate([w_out1[2], w_out2[2]], axis=1)
    else:
        w_dq, w_dk, w_dv = w_out1
    back_w = passed_along(
        jnp.concatenate([w_dk[:WINDOW], w_dv[:WINDOW]], axis=1).astype(jnp.bfloat16), "seq", -1
    ).astype(jnp.float32)
    w_kv = jnp.concatenate([w_dk[WINDOW:], w_dv[WINDOW:]], axis=1)
    w_kv = jnp.concatenate([w_kv[: n - WINDOW], w_kv[n - WINDOW:] + back_w], axis=0)

    both = jnp.concatenate([w_kv, f_final], axis=1)
    peer = lax.ppermute(both, "rep", swap)
    w_sum = (w_kv + peer[:, :2 * cols]).astype(jnp.bfloat16)
    f_other = peer[:, 2 * cols:]
    f_dk_out = jnp.where(first, f_final, f_other).astype(jnp.bfloat16)
    f_dv_out = jnp.where(first, f_other, f_final).astype(jnp.bfloat16)
    return (
        w_dq.reshape(window_query.shape),
        w_sum[:, :cols],
        w_sum[:, cols:],
        f_dq.reshape(full_query.shape),
        f_dk_out,
        f_dv_out,
    )


def solution(mesh):
    placed = (
        P(("groups", "seq")),
        P(("groups", "seq"), "head", "rep"),
        P(("groups", "seq"), "head"),
        P(("groups", "seq"), "head"),
        P(("groups", "seq"), "head", "rep"),
        P("head", "rep"),
        P(("groups", "seq"), "head", "rep"),
        P(("groups", "seq"), "head"),
        P(("groups", "seq"), "head"),
        P(("groups", "seq"), "head", "rep"),
        P("head", "rep"),
    )
    return jax.shard_map(
        body,
        mesh=mesh,
        in_specs=placed,
        out_specs=(
            P(("groups", "seq"), "head", "rep"),
            P(("groups", "seq"), "head"),
            P(("groups", "seq"), "head"),
            P(("groups", "seq"), "head", "rep"),
            P(("groups", "seq"), "head"),
            P(("groups", "seq"), "head"),
        ),
        check_vma=False,
    )
```

```python
import functools
import math

import jax
import jax.numpy as jnp
from jax import lax
from jax.experimental import pallas as pl
from jax.experimental.pallas import tpu as pltpu
from jax.sharding import PartitionSpec as P

HD = 64
WINDOW = 128
NEG = -1e30
NT_DIMS = (((1,), (1,)), ((), ()))


def passed_along(value, axis, steps):
    count = lax.axis_size(axis)
    first, last = (max(0, -steps), min(count, count - steps))
    return lax.ppermute(value, axis, [(source, source + steps) for source in range(first, last)])


def pick_half(block, half):
    return jnp.where(half == 0, block[:, :HD], block[:, HD:])


def attn_bwd_kernel(g0, gn, sink_ref, q_ref, do_ref, k_ref, v_ref, bias_ref, dq_ref, dk_ref, dv_ref):
    g_rel = pl.program_id(0)
    g = g_rel + g0
    i = pl.program_id(1)
    heads = q_ref.shape[1] // HD

    @pl.when((g_rel == 0) & (i == 0))
    def _():
        dk_ref[...] = jnp.zeros_like(dk_ref)
        dv_ref[...] = jnp.zeros_like(dv_ref)

    k = pick_half(k_ref[...], g % 2)
    v = pick_half(v_ref[...], g % 2)
    bias = bias_ref[...]
    dk_acc = None
    dv_acc = None
    dq_parts = []
    for j in range(heads):
        q = q_ref[:, j * HD:(j + 1) * HD]
        do = do_ref[:, j * HD:(j + 1) * HD]
        sink = sink_ref[g, j]
        s = lax.dot_general(q, k, NT_DIMS, preferred_element_type=jnp.float32) + bias
        row_max = jnp.maximum(jnp.max(s, axis=1, keepdims=True), sink)
        e = jnp.exp(s - row_max)
        total = jnp.sum(e, axis=1, keepdims=True) + jnp.exp(sink - row_max)
        p = e * (1.0 / total)
        p_low = p.astype(jnp.bfloat16)
        o = jnp.dot(p_low, v, preferred_element_type=jnp.float32)
        delta = jnp.sum(do.astype(jnp.float32) * o, axis=1, keepdims=True)
        dp = lax.dot_general(do, v, NT_DIMS, preferred_element_type=jnp.float32)
        ds_low = (p * (dp - delta)).astype(jnp.bfloat16)
        dq_parts.append(
            (jnp.dot(ds_low, k, preferred_element_type=jnp.float32) * 0.125).astype(dq_ref.dtype)
        )
        dk = jnp.dot(ds_low.T, q, preferred_element_type=jnp.float32)
        dv = jnp.dot(p_low.T, do, preferred_element_type=jnp.float32)
        dk_acc = dk if dk_acc is None else dk_acc + dk
        dv_acc = dv if dv_acc is None else dv_acc + dv
    dq_ref[...] = jnp.concatenate(dq_parts, axis=1)

    for gg in range(gn):
        @pl.when(g_rel == gg)
        def _():
            dk_ref[:, gg * HD:(gg + 1) * HD] += dk_acc
            dv_ref[:, gg * HD:(gg + 1) * HD] += dv_acc


def attn_bwd(sinks, queries, grads, keys, values, bias, g0, gn):
    n = queries.shape[0]
    m = keys.shape[0]
    heads = sinks.shape[1]
    rows = n
    while rows > 8 and rows * m > (1 << 18):
        rows //= 2
    grid = (gn, n // rows)
    width = heads * HD

    return pl.pallas_call(
        functools.partial(attn_bwd_kernel, g0, gn),
        grid=grid,
        in_specs=[
            pl.BlockSpec(memory_space=pltpu.SMEM),
            pl.BlockSpec((rows, width), lambda g, i: (i, g + g0)),
            pl.BlockSpec((rows, width), lambda g, i: (i, g + g0)),
            pl.BlockSpec((m, 2 * HD), lambda g, i: (0, (g + g0) // 2)),
            pl.BlockSpec((m, 2 * HD), lambda g, i: (0, (g + g0) // 2)),
            pl.BlockSpec((rows, m), lambda g, i: (i, 0)),
        ],
        out_specs=[
            pl.BlockSpec((rows, width), lambda g, i: (i, g)),
            pl.BlockSpec((m, gn * HD), lambda g, i: (0, 0)),
            pl.BlockSpec((m, gn * HD), lambda g, i: (0, 0)),
        ],
        out_shape=[
            jax.ShapeDtypeStruct((n, gn * width), jnp.bfloat16),
            jax.ShapeDtypeStruct((m, gn * HD), jnp.float32),
            jax.ShapeDtypeStruct((m, gn * HD), jnp.float32),
        ],
        compiler_params=pltpu.CompilerParams(
            dimension_semantics=("arbitrary", "arbitrary"),
            vmem_limit_bytes=60 * 1024 * 1024,
        ),
        cost_estimate=pl.CostEstimate(
            flops=12 * gn * heads * n * m * HD,
            transcendentals=gn * heads * n * m,
            bytes_accessed=4 * n * m + 4 * n * gn * heads * HD * 3 + 12 * m * gn * HD,
        ),
    )(sinks, queries, grads, keys, values, bias)


def make_bias(query_pos, query_seg, key_pos, key_seg, window):
    distance = query_pos[:, None] - key_pos[None, :]
    visible = (distance >= 0) & (key_pos[None, :] >= 0) & (query_seg[:, None] == key_seg[None, :])
    if window is not None:
        visible = visible & (distance < window)
    return jnp.where(visible, 0.0, NEG).astype(jnp.float32)


def seg_rows(ids, width):
    count = ids.shape[0]
    lines = -(-count // width)
    flat = jnp.zeros((16 * (-(-lines // 16)) * width,), jnp.bfloat16)
    flat = flat.at[:count].set(ids.astype(jnp.bfloat16))
    return flat.reshape(-1, width)


def read_seg(block, count):
    return block.reshape(-1)[:count].astype(jnp.float32).astype(jnp.int32)


def body(
    segment_ids,
    window_query,
    window_keys,
    window_values,
    window_grad_out,
    window_sinks,
    full_query,
    full_keys,
    full_values,
    full_grad_out,
    full_sinks,
):
    n = window_query.shape[0]
    cols = window_keys.shape[1]
    groups = cols // HD
    seq_count = lax.axis_size("seq")
    seq_index = lax.axis_index("seq")
    rep_index = lax.axis_index("rep")
    first = rep_index == 0
    query_pos = seq_index * n + jnp.arange(n)
    order = list(range(seq_count - 1, 0, -1))
    swap = [(0, 1), (1, 0)]

    halo_in = jnp.concatenate(
        [
            jnp.concatenate([window_keys[n - WINDOW:], window_values[n - WINDOW:]], axis=1),
            seg_rows(segment_ids[n - WINDOW:], 2 * cols),
        ],
        axis=0,
    )
    halo = passed_along(halo_in, "seq", 1)

    own_half = jnp.where(first, full_keys, full_values)
    seg_block = seg_rows(segment_ids, cols)
    payload = jnp.concatenate([own_half, seg_block], axis=0)
    halo, payload = lax.optimization_barrier((halo, payload))
    arrived = [passed_along(payload, "seq", d) for d in order]

    w_keys = jnp.concatenate([halo[:WINDOW, :cols], window_keys], axis=0)
    w_values = jnp.concatenate([halo[:WINDOW, cols:], window_values], axis=0)
    w_seg = jnp.concatenate([read_seg(halo[WINDOW:], WINDOW), segment_ids], axis=0)
    w_pos = seq_index * n - WINDOW + jnp.arange(n + WINDOW)
    w_bias = make_bias(query_pos, segment_ids, w_pos, w_seg, WINDOW)
    w_q = (window_query.reshape(n, -1) * 0.125).astype(jnp.bfloat16)
    w_do = window_grad_out.reshape(n, -1)
    g_split = groups // 2 if groups > 1 else groups
    w_out1 = attn_bwd(window_sinks, w_q, w_do, w_keys, w_values, w_bias, 0, g_split)

    w_out1, arrived = lax.optimization_barrier((w_out1, arrived))
    mine = jnp.concatenate(arrived, axis=0)
    other = lax.ppermute(mine, "rep", swap)
    step = n + seg_block.shape[0]
    key_parts, value_parts, seg_parts = [], [], []
    for idx in range(len(order)):
        a = mine[idx * step:(idx + 1) * step]
        b = other[idx * step:(idx + 1) * step]
        key_parts.append(jnp.where(first, a[:n], b[:n]))
        value_parts.append(jnp.where(first, b[:n], a[:n]))
        seg_parts.append(read_seg(a[n:], n))
    f_keys = jnp.concatenate(key_parts + [full_keys], axis=0)
    f_values = jnp.concatenate(value_parts + [full_values], axis=0)
    f_seg = jnp.concatenate(seg_parts + [segment_ids], axis=0)
    f_pos = (seq_index - (seq_count - 1)) * n + jnp.arange(seq_count * n)
    f_bias = make_bias(query_pos, segment_ids, f_pos, f_seg, None)
    f_q = (full_query.reshape(n, -1) * 0.125).astype(jnp.bfloat16)
    f_do = full_grad_out.reshape(n, -1)
    f_dq, f_dk, f_dv = attn_bwd(full_sinks, f_q, f_do, f_keys, f_values, f_bias, 0, groups)

    give = jnp.where(first, f_dv, f_dk)
    keep = jnp.where(first, f_dk, f_dv)
    summed = keep + lax.ppermute(give, "rep", swap)
    f_final = summed[(seq_count - 1) * n:]
    for jj, d in enumerate(order):
        piece = summed[jj * n:(jj + 1) * n].astype(jnp.bfloat16)
        f_final = f_final + passed_along(piece, "seq", -d).astype(jnp.float32)

    if g_split < groups:
        w_out2 = attn_bwd(window_sinks, w_q, w_do, w_keys, w_values, w_bias, g_split, groups - g_split)
        w_dq = jnp.concatenate([w_out1[0], w_out2[0]], axis=1)
        w_dk = jnp.concatenate([w_out1[1], w_out2[1]], axis=1)
        w_dv = jnp.concatenate([w_out1[2], w_out2[2]], axis=1)
    else:
        w_dq, w_dk, w_dv = w_out1
    back_w = passed_along(
        jnp.concatenate([w_dk[:WINDOW], w_dv[:WINDOW]], axis=1).astype(jnp.bfloat16), "seq", -1
    ).astype(jnp.float32)
    w_kv = jnp.concatenate([w_dk[WINDOW:], w_dv[WINDOW:]], axis=1)
    w_kv = jnp.concatenate([w_kv[: n - WINDOW], w_kv[n - WINDOW:] + back_w], axis=0)

    both = jnp.concatenate([w_kv, f_final], axis=1)
    peer = lax.ppermute(both, "rep", swap)
    w_sum = (w_kv + peer[:, :2 * cols]).astype(jnp.bfloat16)
    f_other = peer[:, 2 * cols:]
    f_dk_out = jnp.where(first, f_final, f_other).astype(jnp.bfloat16)
    f_dv_out = jnp.where(first, f_other, f_final).astype(jnp.bfloat16)
    return (
        w_dq.reshape(window_query.shape),
        w_sum[:, :cols],
        w_sum[:, cols:],
        f_dq.reshape(full_query.shape),
        f_dk_out,
        f_dv_out,
    )


def solution(mesh):
    placed = (
        P(("groups", "seq")),
        P(("groups", "seq"), "head", "rep"),
        P(("groups", "seq"), "head"),
        P(("groups", "seq"), "head"),
        P(("groups", "seq"), "head", "rep"),
        P("head", "rep"),
        P(("groups", "seq"), "head", "rep"),
        P(("groups", "seq"), "head"),
        P(("groups", "seq"), "head"),
        P(("groups", "seq"), "head", "rep"),
        P("head", "rep"),
    )
    return jax.shard_map(
        body,
        mesh=mesh,
        in_specs=placed,
        out_specs=(
            P(("groups", "seq"), "head", "rep"),
            P(("groups", "seq"), "head"),
            P(("groups", "seq"), "head"),
            P(("groups", "seq"), "head", "rep"),
            P(("groups", "seq"), "head"),
            P(("groups", "seq"), "head"),
        ),
        check_vma=False,
    )
```

```python
import functools
import math

import jax
import jax.numpy as jnp
from jax import lax
from jax.experimental import pallas as pl
from jax.experimental.pallas import tpu as pltpu
from jax.sharding import PartitionSpec as P

HD = 64
WINDOW = 128
NEG = -1e30
NT_DIMS = (((1,), (1,)), ((), ()))


def passed_along(value, axis, steps):
    count = lax.axis_size(axis)
    first, last = (max(0, -steps), min(count, count - steps))
    return lax.ppermute(value, axis, [(source, source + steps) for source in range(first, last)])


def pick_half(block, half):
    return jnp.where(half == 0, block[:, :HD], block[:, HD:])


def attn_bwd_kernel(g0, gn, sink_ref, q_ref, do_ref, k_ref, v_ref, bias_ref, dq_ref, dk_ref, dv_ref):
    g_rel = pl.program_id(0)
    g = g_rel + g0
    i = pl.program_id(1)
    heads = q_ref.shape[1] // HD

    @pl.when((g_rel == 0) & (i == 0))
    def _():
        dk_ref[...] = jnp.zeros_like(dk_ref)
        dv_ref[...] = jnp.zeros_like(dv_ref)

    k = pick_half(k_ref[...], g % 2)
    v = pick_half(v_ref[...], g % 2)
    bias = bias_ref[...]
    dk_acc = None
    dv_acc = None
    dq_parts = []
    for j in range(heads):
        q = q_ref[:, j * HD:(j + 1) * HD]
        do = do_ref[:, j * HD:(j + 1) * HD]
        sink = sink_ref[g, j]
        s = lax.dot_general(q, k, NT_DIMS, preferred_element_type=jnp.float32) + bias
        row_max = jnp.maximum(jnp.max(s, axis=1, keepdims=True), sink)
        e = jnp.exp(s - row_max)
        total = jnp.sum(e, axis=1, keepdims=True) + jnp.exp(sink - row_max)
        p = e * (1.0 / total)
        p_low = p.astype(jnp.bfloat16)
        o = jnp.dot(p_low, v, preferred_element_type=jnp.float32)
        delta = jnp.sum(do.astype(jnp.float32) * o, axis=1, keepdims=True)
        dp = lax.dot_general(do, v, NT_DIMS, preferred_element_type=jnp.float32)
        ds_low = (p * (dp - delta)).astype(jnp.bfloat16)
        dq_parts.append(
            (jnp.dot(ds_low, k, preferred_element_type=jnp.float32) * 0.125).astype(dq_ref.dtype)
        )
        dk = jnp.dot(ds_low.T, q, preferred_element_type=jnp.float32)
        dv = jnp.dot(p_low.T, do, preferred_element_type=jnp.float32)
        dk_acc = dk if dk_acc is None else dk_acc + dk
        dv_acc = dv if dv_acc is None else dv_acc + dv
    dq_ref[...] = jnp.concatenate(dq_parts, axis=1)

    for gg in range(gn):
        @pl.when(g_rel == gg)
        def _():
            dk_ref[:, gg * HD:(gg + 1) * HD] += dk_acc
            dv_ref[:, gg * HD:(gg + 1) * HD] += dv_acc


def attn_bwd(sinks, queries, grads, keys, values, bias, g0, gn):
    n = queries.shape[0]
    m = keys.shape[0]
    heads = sinks.shape[1]
    rows = n
    while rows > 8 and rows * m > (1 << 18):
        rows //= 2
    grid = (gn, n // rows)
    width = heads * HD

    return pl.pallas_call(
        functools.partial(attn_bwd_kernel, g0, gn),
        grid=grid,
        in_specs=[
            pl.BlockSpec(memory_space=pltpu.SMEM),
            pl.BlockSpec((rows, width), lambda g, i: (i, g + g0)),
            pl.BlockSpec((rows, width), lambda g, i: (i, g + g0)),
            pl.BlockSpec((m, 2 * HD), lambda g, i: (0, (g + g0) // 2)),
            pl.BlockSpec((m, 2 * HD), lambda g, i: (0, (g + g0) // 2)),
            pl.BlockSpec((rows, m), lambda g, i: (i, 0)),
        ],
        out_specs=[
            pl.BlockSpec((rows, width), lambda g, i: (i, g)),
            pl.BlockSpec((m, gn * HD), lambda g, i: (0, 0)),
            pl.BlockSpec((m, gn * HD), lambda g, i: (0, 0)),
        ],
        out_shape=[
            jax.ShapeDtypeStruct((n, gn * width), jnp.bfloat16),
            jax.ShapeDtypeStruct((m, gn * HD), jnp.float32),
            jax.ShapeDtypeStruct((m, gn * HD), jnp.float32),
        ],
        compiler_params=pltpu.CompilerParams(
            dimension_semantics=("arbitrary", "arbitrary"),
            vmem_limit_bytes=60 * 1024 * 1024,
        ),
        cost_estimate=pl.CostEstimate(
            flops=12 * gn * heads * n * m * HD,
            transcendentals=gn * heads * n * m,
            bytes_accessed=4 * n * m + 4 * n * gn * heads * HD * 3 + 12 * m * gn * HD,
        ),
    )(sinks, queries, grads, keys, values, bias)


def make_bias(query_pos, query_seg, key_pos, key_seg, window):
    distance = query_pos[:, None] - key_pos[None, :]
    visible = (distance >= 0) & (key_pos[None, :] >= 0) & (query_seg[:, None] == key_seg[None, :])
    if window is not None:
        visible = visible & (distance < window)
    return jnp.where(visible, 0.0, NEG).astype(jnp.float32)


def seg_rows(ids, width):
    count = ids.shape[0]
    lines = -(-count // width)
    flat = jnp.zeros((16 * (-(-lines // 16)) * width,), jnp.bfloat16)
    flat = flat.at[:count].set(ids.astype(jnp.bfloat16))
    return flat.reshape(-1, width)


def read_seg(block, count):
    return block.reshape(-1)[:count].astype(jnp.float32).astype(jnp.int32)


def body(
    segment_ids,
    window_query,
    window_keys,
    window_values,
    window_grad_out,
    window_sinks,
    full_query,
    full_keys,
    full_values,
    full_grad_out,
    full_sinks,
):
    n = window_query.shape[0]
    cols = window_keys.shape[1]
    groups = cols // HD
    seq_count = lax.axis_size("seq")
    seq_index = lax.axis_index("seq")
    rep_index = lax.axis_index("rep")
    first = rep_index == 0
    query_pos = seq_index * n + jnp.arange(n)
    order = list(range(seq_count - 1, 0, -1))
    swap = [(0, 1), (1, 0)]

    halo_in = jnp.concatenate(
        [
            jnp.concatenate([window_keys[n - WINDOW:], window_values[n - WINDOW:]], axis=1),
            seg_rows(segment_ids[n - WINDOW:], 2 * cols),
        ],
        axis=0,
    )
    halo = passed_along(halo_in, "seq", 1)

    own_half = jnp.where(first, full_keys, full_values)
    seg_block = seg_rows(segment_ids, cols)
    payload = jnp.concatenate([own_half, seg_block], axis=0)
    halo, payload = lax.optimization_barrier((halo, payload))
    arrived = [passed_along(payload, "seq", d) for d in order]

    w_keys = jnp.concatenate([halo[:WINDOW, :cols], window_keys], axis=0)
    w_values = jnp.concatenate([halo[:WINDOW, cols:], window_values], axis=0)
    w_seg = jnp.concatenate([read_seg(halo[WINDOW:], WINDOW), segment_ids], axis=0)
    w_pos = seq_index * n - WINDOW + jnp.arange(n + WINDOW)
    w_bias = make_bias(query_pos, segment_ids, w_pos, w_seg, WINDOW)
    w_q = (window_query.reshape(n, -1) * 0.125).astype(jnp.bfloat16)
    w_do = window_grad_out.reshape(n, -1)
    g_split = groups // 2 if groups > 1 else groups
    w_out1 = attn_bwd(window_sinks, w_q, w_do, w_keys, w_values, w_bias, 0, g_split)

    w_out1, arrived = lax.optimization_barrier((w_out1, arrived))
    mine = jnp.concatenate(arrived, axis=0)
    other = lax.ppermute(mine, "rep", swap)
    step = n + seg_block.shape[0]
    key_parts, value_parts, seg_parts = [], [], []
    for idx in range(len(order)):
        a = mine[idx * step:(idx + 1) * step]
        b = other[idx * step:(idx + 1) * step]
        key_parts.append(jnp.where(first, a[:n], b[:n]))
        value_parts.append(jnp.where(first, b[:n], a[:n]))
        seg_parts.append(read_seg(a[n:], n))
    f_keys = jnp.concatenate(key_parts + [full_keys], axis=0)
    f_values = jnp.concatenate(value_parts + [full_values], axis=0)
    f_seg = jnp.concatenate(seg_parts + [segment_ids], axis=0)
    f_pos = (seq_index - (seq_count - 1)) * n + jnp.arange(seq_count * n)
    f_bias = make_bias(query_pos, segment_ids, f_pos, f_seg, None)
    f_q = (full_query.reshape(n, -1) * 0.125).astype(jnp.bfloat16)
    f_do = full_grad_out.reshape(n, -1)
    f_dq, f_dk, f_dv = attn_bwd(full_sinks, f_q, f_do, f_keys, f_values, f_bias, 0, groups)

    summed = jnp.concatenate([f_dk, f_dv], axis=1)
    returned = [
        passed_along(summed[jj * n:(jj + 1) * n].astype(jnp.bfloat16), "seq", -d)
        for jj, d in enumerate(order)
    ]
    if g_split < groups:
        summed, w_q = lax.optimization_barrier((summed, w_q))
        w_out2 = attn_bwd(window_sinks, w_q, w_do, w_keys, w_values, w_bias, g_split, groups - g_split)
        w_dq = jnp.concatenate([w_out1[0], w_out2[0]], axis=1)
        w_dk = jnp.concatenate([w_out1[1], w_out2[1]], axis=1)
        w_dv = jnp.concatenate([w_out1[2], w_out2[2]], axis=1)
    else:
        w_dq, w_dk, w_dv = w_out1
    w_dk, returned = lax.optimization_barrier((w_dk, returned))
    f_final = summed[(seq_count - 1) * n:]
    for piece in returned:
        f_final = f_final + piece.astype(jnp.float32)
    back_w = passed_along(
        jnp.concatenate([w_dk[:WINDOW], w_dv[:WINDOW]], axis=1).astype(jnp.bfloat16), "seq", -1
    ).astype(jnp.float32)
    w_kv = jnp.concatenate([w_dk[WINDOW:], w_dv[WINDOW:]], axis=1)
    w_kv = jnp.concatenate([w_kv[: n - WINDOW], w_kv[n - WINDOW:] + back_w], axis=0)

    both = jnp.concatenate([w_kv, f_final], axis=1)
    both = (both + lax.ppermute(both, "rep", swap)).astype(jnp.bfloat16)
    w_sum = both[:, :2 * cols]
    f_dk_out = both[:, 2 * cols:3 * cols]
    f_dv_out = both[:, 3 * cols:]
    return (
        w_dq.reshape(window_query.shape),
        w_sum[:, :cols],
        w_sum[:, cols:],
        f_dq.reshape(full_query.shape),
        f_dk_out,
        f_dv_out,
    )


def solution(mesh):
    placed = (
        P(("groups", "seq")),
        P(("groups", "seq"), "head", "rep"),
        P(("groups", "seq"), "head"),
        P(("groups", "seq"), "head"),
        P(("groups", "seq"), "head", "rep"),
        P("head", "rep"),
        P(("groups", "seq"), "head", "rep"),
        P(("groups", "seq"), "head"),
        P(("groups", "seq"), "head"),
        P(("groups", "seq"), "head", "rep"),
        P("head", "rep"),
    )
    return jax.shard_map(
        body,
        mesh=mesh,
        in_specs=placed,
        out_specs=(
            P(("groups", "seq"), "head", "rep"),
            P(("groups", "seq"), "head"),
            P(("groups", "seq"), "head"),
            P(("groups", "seq"), "head", "rep"),
            P(("groups", "seq"), "head"),
            P(("groups", "seq"), "head"),
        ),
        check_vma=False,
    )
```

```python
import functools
import math

import jax
import jax.numpy as jnp
from jax import lax
from jax.experimental import pallas as pl
from jax.experimental.pallas import tpu as pltpu
from jax.sharding import PartitionSpec as P

HD = 64
WINDOW = 128
NEG = -1e30
NT_DIMS = (((1,), (1,)), ((), ()))


def passed_along(value, axis, steps):
    count = lax.axis_size(axis)
    first, last = (max(0, -steps), min(count, count - steps))
    return lax.ppermute(value, axis, [(source, source + steps) for source in range(first, last)])


def pick_half(block, half):
    return jnp.where(half == 0, block[:, :HD], block[:, HD:])


def attn_bwd_kernel(g0, gn, sink_ref, q_ref, do_ref, k_ref, v_ref, bias_ref, dq_ref, dk_ref, dv_ref):
    g_rel = pl.program_id(0)
    g = g_rel + g0
    i = pl.program_id(1)
    heads = q_ref.shape[1] // HD

    @pl.when((g_rel == 0) & (i == 0))
    def _():
        dk_ref[...] = jnp.zeros_like(dk_ref)
        dv_ref[...] = jnp.zeros_like(dv_ref)

    k = pick_half(k_ref[...], g % 2)
    v = pick_half(v_ref[...], g % 2)
    bias = bias_ref[...]
    dk_acc = None
    dv_acc = None
    dq_parts = []
    for j in range(heads):
        q = q_ref[:, j * HD:(j + 1) * HD]
        do = do_ref[:, j * HD:(j + 1) * HD]
        sink = sink_ref[g, j]
        s = lax.dot_general(q, k, NT_DIMS, preferred_element_type=jnp.float32) + bias
        row_max = jnp.maximum(jnp.max(s, axis=1, keepdims=True), sink)
        e = jnp.exp(s - row_max)
        total = jnp.sum(e, axis=1, keepdims=True) + jnp.exp(sink - row_max)
        p = e * (1.0 / total)
        p_low = p.astype(jnp.bfloat16)
        dp = lax.dot_general(do, v, NT_DIMS, preferred_element_type=jnp.float32)
        delta = jnp.sum(p_low.astype(jnp.float32) * dp, axis=1, keepdims=True)
        ds_low = (p * (dp - delta)).astype(jnp.bfloat16)
        dq_parts.append(
            (jnp.dot(ds_low, k, preferred_element_type=jnp.float32) * 0.125).astype(dq_ref.dtype)
        )
        dk = jnp.dot(ds_low.T, q, preferred_element_type=jnp.float32)
        dv = jnp.dot(p_low.T, do, preferred_element_type=jnp.float32)
        dk_acc = dk if dk_acc is None else dk_acc + dk
        dv_acc = dv if dv_acc is None else dv_acc + dv
    dq_ref[...] = jnp.concatenate(dq_parts, axis=1)

    for gg in range(gn):
        @pl.when(g_rel == gg)
        def _():
            dk_ref[:, gg * HD:(gg + 1) * HD] += dk_acc
            dv_ref[:, gg * HD:(gg + 1) * HD] += dv_acc


def attn_bwd(sinks, queries, grads, keys, values, bias, g0, gn):
    n = queries.shape[0]
    m = keys.shape[0]
    heads = sinks.shape[1]
    rows = n
    while rows > 8 and rows * m > (1 << 18):
        rows //= 2
    grid = (gn, n // rows)
    width = heads * HD

    return pl.pallas_call(
        functools.partial(attn_bwd_kernel, g0, gn),
        grid=grid,
        in_specs=[
            pl.BlockSpec(memory_space=pltpu.SMEM),
            pl.BlockSpec((rows, width), lambda g, i: (i, g + g0)),
            pl.BlockSpec((rows, width), lambda g, i: (i, g + g0)),
            pl.BlockSpec((m, 2 * HD), lambda g, i: (0, (g + g0) // 2)),
            pl.BlockSpec((m, 2 * HD), lambda g, i: (0, (g + g0) // 2)),
            pl.BlockSpec((rows, m), lambda g, i: (i, 0)),
        ],
        out_specs=[
            pl.BlockSpec((rows, width), lambda g, i: (i, g)),
            pl.BlockSpec((m, gn * HD), lambda g, i: (0, 0)),
            pl.BlockSpec((m, gn * HD), lambda g, i: (0, 0)),
        ],
        out_shape=[
            jax.ShapeDtypeStruct((n, gn * width), jnp.bfloat16),
            jax.ShapeDtypeStruct((m, gn * HD), jnp.float32),
            jax.ShapeDtypeStruct((m, gn * HD), jnp.float32),
        ],
        compiler_params=pltpu.CompilerParams(
            dimension_semantics=("arbitrary", "arbitrary"),
            vmem_limit_bytes=60 * 1024 * 1024,
        ),
        cost_estimate=pl.CostEstimate(
            flops=10 * gn * heads * n * m * HD,
            transcendentals=gn * heads * n * m,
            bytes_accessed=4 * n * m + 4 * n * gn * heads * HD * 3 + 12 * m * gn * HD,
        ),
    )(sinks, queries, grads, keys, values, bias)


def make_bias(query_pos, query_seg, key_pos, key_seg, window):
    distance = query_pos[:, None] - key_pos[None, :]
    visible = (distance >= 0) & (key_pos[None, :] >= 0) & (query_seg[:, None] == key_seg[None, :])
    if window is not None:
        visible = visible & (distance < window)
    return jnp.where(visible, 0.0, NEG).astype(jnp.float32)


def seg_rows(ids, width):
    count = ids.shape[0]
    lines = -(-count // width)
    flat = jnp.zeros((16 * (-(-lines // 16)) * width,), jnp.bfloat16)
    flat = flat.at[:count].set(ids.astype(jnp.bfloat16))
    return flat.reshape(-1, width)


def read_seg(block, count):
    return block.reshape(-1)[:count].astype(jnp.float32).astype(jnp.int32)


def body(
    segment_ids,
    window_query,
    window_keys,
    window_values,
    window_grad_out,
    window_sinks,
    full_query,
    full_keys,
    full_values,
    full_grad_out,
    full_sinks,
):
    n = window_query.shape[0]
    cols = window_keys.shape[1]
    groups = cols // HD
    seq_count = lax.axis_size("seq")
    seq_index = lax.axis_index("seq")
    rep_index = lax.axis_index("rep")
    first = rep_index == 0
    query_pos = seq_index * n + jnp.arange(n)
    order = list(range(seq_count - 1, 0, -1))
    swap = [(0, 1), (1, 0)]

    halo_in = jnp.concatenate(
        [
            jnp.concatenate([window_keys[n - WINDOW:], window_values[n - WINDOW:]], axis=1),
            seg_rows(segment_ids[n - WINDOW:], 2 * cols),
        ],
        axis=0,
    )
    halo = passed_along(halo_in, "seq", 1)

    own_half = jnp.where(first, full_keys, full_values)
    seg_block = seg_rows(segment_ids, cols)
    payload = jnp.concatenate([own_half, seg_block], axis=0)
    halo, payload = lax.optimization_barrier((halo, payload))
    arrived = [passed_along(payload, "seq", d) for d in order]

    w_keys = jnp.concatenate([halo[:WINDOW, :cols], window_keys], axis=0)
    w_values = jnp.concatenate([halo[:WINDOW, cols:], window_values], axis=0)
    w_seg = jnp.concatenate([read_seg(halo[WINDOW:], WINDOW), segment_ids], axis=0)
    w_pos = seq_index * n - WINDOW + jnp.arange(n + WINDOW)
    w_bias = make_bias(query_pos, segment_ids, w_pos, w_seg, WINDOW)
    w_q = (window_query.reshape(n, -1) * 0.125).astype(jnp.bfloat16)
    w_do = window_grad_out.reshape(n, -1)
    g_split = groups // 2 if groups > 1 else groups
    w_out1 = attn_bwd(window_sinks, w_q, w_do, w_keys, w_values, w_bias, 0, g_split)

    w_out1, arrived = lax.optimization_barrier((w_out1, arrived))
    mine = jnp.concatenate(arrived, axis=0)
    other = lax.ppermute(mine, "rep", swap)
    step = n + seg_block.shape[0]
    key_parts, value_parts, seg_parts = [], [], []
    for idx in range(len(order)):
        a = mine[idx * step:(idx + 1) * step]
        b = other[idx * step:(idx + 1) * step]
        key_parts.append(jnp.where(first, a[:n], b[:n]))
        value_parts.append(jnp.where(first, b[:n], a[:n]))
        seg_parts.append(read_seg(a[n:], n))
    f_keys = jnp.concatenate(key_parts + [full_keys], axis=0)
    f_values = jnp.concatenate(value_parts + [full_values], axis=0)
    f_seg = jnp.concatenate(seg_parts + [segment_ids], axis=0)
    f_pos = (seq_index - (seq_count - 1)) * n + jnp.arange(seq_count * n)
    f_bias = make_bias(query_pos, segment_ids, f_pos, f_seg, None)
    f_q = (full_query.reshape(n, -1) * 0.125).astype(jnp.bfloat16)
    f_do = full_grad_out.reshape(n, -1)
    f_dq, f_dk, f_dv = attn_bwd(full_sinks, f_q, f_do, f_keys, f_values, f_bias, 0, groups)

    give = jnp.where(first, f_dv, f_dk)
    keep = jnp.where(first, f_dk, f_dv)
    summed = keep + lax.ppermute(give, "rep", swap)
    f_final = summed[(seq_count - 1) * n:]
    for jj, d in enumerate(order):
        piece = summed[jj * n:(jj + 1) * n].astype(jnp.bfloat16)
        f_final = f_final + passed_along(piece, "seq", -d).astype(jnp.float32)

    if g_split < groups:
        w_out2 = attn_bwd(window_sinks, w_q, w_do, w_keys, w_values, w_bias, g_split, groups - g_split)
        w_dq = jnp.concatenate([w_out1[0], w_out2[0]], axis=1)
        w_dk = jnp.concatenate([w_out1[1], w_out2[1]], axis=1)
        w_dv = jnp.concatenate([w_out1[2], w_out2[2]], axis=1)
    else:
        w_dq, w_dk, w_dv = w_out1
    back_w = passed_along(
        jnp.concatenate([w_dk[:WINDOW], w_dv[:WINDOW]], axis=1).astype(jnp.bfloat16), "seq", -1
    ).astype(jnp.float32)
    w_kv = jnp.concatenate([w_dk[WINDOW:], w_dv[WINDOW:]], axis=1)
    w_kv = jnp.concatenate([w_kv[: n - WINDOW], w_kv[n - WINDOW:] + back_w], axis=0)

    both = jnp.concatenate([w_kv, f_final], axis=1)
    peer = lax.ppermute(both, "rep", swap)
    w_sum = (w_kv + peer[:, :2 * cols]).astype(jnp.bfloat16)
    f_other = peer[:, 2 * cols:]
    f_dk_out = jnp.where(first, f_final, f_other).astype(jnp.bfloat16)
    f_dv_out = jnp.where(first, f_other, f_final).astype(jnp.bfloat16)
    return (
        w_dq.reshape(window_query.shape),
        w_sum[:, :cols],
        w_sum[:, cols:],
        f_dq.reshape(full_query.shape),
        f_dk_out,
        f_dv_out,
    )


def solution(mesh):
    placed = (
        P(("groups", "seq")),
        P(("groups", "seq"), "head", "rep"),
        P(("groups", "seq"), "head"),
        P(("groups", "seq"), "head"),
        P(("groups", "seq"), "head", "rep"),
        P("head", "rep"),
        P(("groups", "seq"), "head", "rep"),
        P(("groups", "seq"), "head"),
        P(("groups", "seq"), "head"),
        P(("groups", "seq"), "head", "rep"),
        P("head", "rep"),
    )
    return jax.shard_map(
        body,
        mesh=mesh,
        in_specs=placed,
        out_specs=(
            P(("groups", "seq"), "head", "rep"),
            P(("groups", "seq"), "head"),
            P(("groups", "seq"), "head"),
            P(("groups", "seq"), "head", "rep"),
            P(("groups", "seq"), "head"),
            P(("groups", "seq"), "head"),
        ),
        check_vma=False,
    )
```

```python
import functools
import math

import jax
import jax.numpy as jnp
from jax import lax
from jax.experimental import pallas as pl
from jax.experimental.pallas import tpu as pltpu
from jax.sharding import PartitionSpec as P

HD = 64
WINDOW = 128
NEG = -1e30
NT_DIMS = (((1,), (1,)), ((), ()))


def passed_along(value, axis, steps):
    count = lax.axis_size(axis)
    first, last = (max(0, -steps), min(count, count - steps))
    return lax.ppermute(value, axis, [(source, source + steps) for source in range(first, last)])


def pick_half(block, half):
    return jnp.where(half == 0, block[:, :HD], block[:, HD:])


def attn_bwd_kernel(g0, gn, sink_ref, q_ref, do_ref, k_ref, v_ref, bias_ref, dq_ref, dk_ref, dv_ref):
    g_rel = pl.program_id(0)
    g = g_rel + g0
    i = pl.program_id(1)
    heads = q_ref.shape[1] // HD

    @pl.when((g_rel == 0) & (i == 0))
    def _():
        dk_ref[...] = jnp.zeros_like(dk_ref)
        dv_ref[...] = jnp.zeros_like(dv_ref)

    k = pick_half(k_ref[...], g % 2)
    v = pick_half(v_ref[...], g % 2)
    bias = bias_ref[...]
    rows, m = bias.shape
    q = jnp.concatenate([q_ref[:, j * HD:(j + 1) * HD] for j in range(heads)], axis=0)
    do = jnp.concatenate([do_ref[:, j * HD:(j + 1) * HD] for j in range(heads)], axis=0)
    sink = jnp.concatenate(
        [jnp.full((rows, 1), sink_ref[g, j], jnp.float32) for j in range(heads)], axis=0
    )
    s = lax.dot_general(q, k, NT_DIMS, preferred_element_type=jnp.float32)
    s = (s.reshape(heads, rows, m) + bias[None]).reshape(heads * rows, m)
    row_max = jnp.maximum(jnp.max(s, axis=1, keepdims=True), sink)
    e = jnp.exp(s - row_max)
    total = jnp.sum(e, axis=1, keepdims=True) + jnp.exp(sink - row_max)
    p = e * (1.0 / total)
    p_low = p.astype(jnp.bfloat16)
    dp = lax.dot_general(do, v, NT_DIMS, preferred_element_type=jnp.float32)
    delta = jnp.sum(p_low.astype(jnp.float32) * dp, axis=1, keepdims=True)
    ds_low = (p * (dp - delta)).astype(jnp.bfloat16)
    dq = (jnp.dot(ds_low, k, preferred_element_type=jnp.float32) * 0.125).astype(dq_ref.dtype)
    dq_ref[...] = jnp.concatenate([dq[j * rows:(j + 1) * rows] for j in range(heads)], axis=1)
    dk_acc = jnp.dot(ds_low.T, q, preferred_element_type=jnp.float32)
    dv_acc = jnp.dot(p_low.T, do, preferred_element_type=jnp.float32)

    for gg in range(gn):
        @pl.when(g_rel == gg)
        def _():
            dk_ref[:, gg * HD:(gg + 1) * HD] += dk_acc
            dv_ref[:, gg * HD:(gg + 1) * HD] += dv_acc


def attn_bwd(sinks, queries, grads, keys, values, bias, g0, gn):
    n = queries.shape[0]
    m = keys.shape[0]
    heads = sinks.shape[1]
    rows = n
    while rows > 8 and heads * rows * m > (1 << 20):
        rows //= 2
    grid = (gn, n // rows)
    width = heads * HD

    return pl.pallas_call(
        functools.partial(attn_bwd_kernel, g0, gn),
        grid=grid,
        in_specs=[
            pl.BlockSpec(memory_space=pltpu.SMEM),
            pl.BlockSpec((rows, width), lambda g, i: (i, g + g0)),
            pl.BlockSpec((rows, width), lambda g, i: (i, g + g0)),
            pl.BlockSpec((m, 2 * HD), lambda g, i: (0, (g + g0) // 2)),
            pl.BlockSpec((m, 2 * HD), lambda g, i: (0, (g + g0) // 2)),
            pl.BlockSpec((rows, m), lambda g, i: (i, 0)),
        ],
        out_specs=[
            pl.BlockSpec((rows, width), lambda g, i: (i, g)),
            pl.BlockSpec((m, gn * HD), lambda g, i: (0, 0)),
            pl.BlockSpec((m, gn * HD), lambda g, i: (0, 0)),
        ],
        out_shape=[
            jax.ShapeDtypeStruct((n, gn * width), jnp.bfloat16),
            jax.ShapeDtypeStruct((m, gn * HD), jnp.float32),
            jax.ShapeDtypeStruct((m, gn * HD), jnp.float32),
        ],
        compiler_params=pltpu.CompilerParams(
            dimension_semantics=("arbitrary", "arbitrary"),
            vmem_limit_bytes=60 * 1024 * 1024,
        ),
        cost_estimate=pl.CostEstimate(
            flops=10 * gn * heads * n * m * HD,
            transcendentals=gn * heads * n * m,
            bytes_accessed=4 * n * m + 4 * n * gn * heads * HD * 3 + 12 * m * gn * HD,
        ),
    )(sinks, queries, grads, keys, values, bias)


def make_bias(query_pos, query_seg, key_pos, key_seg, window):
    distance = query_pos[:, None] - key_pos[None, :]
    visible = (distance >= 0) & (key_pos[None, :] >= 0) & (query_seg[:, None] == key_seg[None, :])
    if window is not None:
        visible = visible & (distance < window)
    return jnp.where(visible, 0.0, NEG).astype(jnp.float32)


def seg_rows(ids, width):
    count = ids.shape[0]
    lines = -(-count // width)
    flat = jnp.zeros((16 * (-(-lines // 16)) * width,), jnp.bfloat16)
    flat = flat.at[:count].set(ids.astype(jnp.bfloat16))
    return flat.reshape(-1, width)


def read_seg(block, count):
    return block.reshape(-1)[:count].astype(jnp.float32).astype(jnp.int32)


def body(
    segment_ids,
    window_query,
    window_keys,
    window_values,
    window_grad_out,
    window_sinks,
    full_query,
    full_keys,
    full_values,
    full_grad_out,
    full_sinks,
):
    n = window_query.shape[0]
    cols = window_keys.shape[1]
    groups = cols // HD
    seq_count = lax.axis_size("seq")
    seq_index = lax.axis_index("seq")
    rep_index = lax.axis_index("rep")
    first = rep_index == 0
    query_pos = seq_index * n + jnp.arange(n)
    order = list(range(seq_count - 1, 0, -1))
    swap = [(0, 1), (1, 0)]

    halo_in = jnp.concatenate(
        [
            jnp.concatenate([window_keys[n - WINDOW:], window_values[n - WINDOW:]], axis=1),
            seg_rows(segment_ids[n - WINDOW:], 2 * cols),
        ],
        axis=0,
    )
    halo = passed_along(halo_in, "seq", 1)

    own_half = jnp.where(first, full_keys, full_values)
    seg_block = seg_rows(segment_ids, cols)
    payload = jnp.concatenate([own_half, seg_block], axis=0)
    halo, payload = lax.optimization_barrier((halo, payload))
    arrived = [passed_along(payload, "seq", d) for d in order]

    w_keys = jnp.concatenate([halo[:WINDOW, :cols], window_keys], axis=0)
    w_values = jnp.concatenate([halo[:WINDOW, cols:], window_values], axis=0)
    w_seg = jnp.concatenate([read_seg(halo[WINDOW:], WINDOW), segment_ids], axis=0)
    w_pos = seq_index * n - WINDOW + jnp.arange(n + WINDOW)
    w_bias = make_bias(query_pos, segment_ids, w_pos, w_seg, WINDOW)
    w_q = (window_query.reshape(n, -1) * 0.125).astype(jnp.bfloat16)
    w_do = window_grad_out.reshape(n, -1)
    g_split = groups // 2 if groups > 1 else groups
    w_out1 = attn_bwd(window_sinks, w_q, w_do, w_keys, w_values, w_bias, 0, g_split)

    w_out1, arrived = lax.optimization_barrier((w_out1, arrived))
    mine = jnp.concatenate(arrived, axis=0)
    other = lax.ppermute(mine, "rep", swap)
    step = n + seg_block.shape[0]
    key_parts, value_parts, seg_parts = [], [], []
    for idx in range(len(order)):
        a = mine[idx * step:(idx + 1) * step]
        b = other[idx * step:(idx + 1) * step]
        key_parts.append(jnp.where(first, a[:n], b[:n]))
        value_parts.append(jnp.where(first, b[:n], a[:n]))
        seg_parts.append(read_seg(a[n:], n))
    f_keys = jnp.concatenate(key_parts + [full_keys], axis=0)
    f_values = jnp.concatenate(value_parts + [full_values], axis=0)
    f_seg = jnp.concatenate(seg_parts + [segment_ids], axis=0)
    f_pos = (seq_index - (seq_count - 1)) * n + jnp.arange(seq_count * n)
    f_bias = make_bias(query_pos, segment_ids, f_pos, f_seg, None)
    f_q = (full_query.reshape(n, -1) * 0.125).astype(jnp.bfloat16)
    f_do = full_grad_out.reshape(n, -1)
    f_dq, f_dk, f_dv = attn_bwd(full_sinks, f_q, f_do, f_keys, f_values, f_bias, 0, groups)

    give = jnp.where(first, f_dv, f_dk)
    keep = jnp.where(first, f_dk, f_dv)
    summed = keep + lax.ppermute(give, "rep", swap)
    f_final = summed[(seq_count - 1) * n:]
    for jj, d in enumerate(order):
        piece = summed[jj * n:(jj + 1) * n].astype(jnp.bfloat16)
        f_final = f_final + passed_along(piece, "seq", -d).astype(jnp.float32)

    if g_split < groups:
        w_out2 = attn_bwd(window_sinks, w_q, w_do, w_keys, w_values, w_bias, g_split, groups - g_split)
        w_dq = jnp.concatenate([w_out1[0], w_out2[0]], axis=1)
        w_dk = jnp.concatenate([w_out1[1], w_out2[1]], axis=1)
        w_dv = jnp.concatenate([w_out1[2], w_out2[2]], axis=1)
    else:
        w_dq, w_dk, w_dv = w_out1
    back_w = passed_along(
        jnp.concatenate([w_dk[:WINDOW], w_dv[:WINDOW]], axis=1).astype(jnp.bfloat16), "seq", -1
    ).astype(jnp.float32)
    w_kv = jnp.concatenate([w_dk[WINDOW:], w_dv[WINDOW:]], axis=1)
    w_kv = jnp.concatenate([w_kv[: n - WINDOW], w_kv[n - WINDOW:] + back_w], axis=0)

    both = jnp.concatenate([w_kv, f_final], axis=1)
    peer = lax.ppermute(both, "rep", swap)
    w_sum = (w_kv + peer[:, :2 * cols]).astype(jnp.bfloat16)
    f_other = peer[:, 2 * cols:]
    f_dk_out = jnp.where(first, f_final, f_other).astype(jnp.bfloat16)
    f_dv_out = jnp.where(first, f_other, f_final).astype(jnp.bfloat16)
    return (
        w_dq.reshape(window_query.shape),
        w_sum[:, :cols],
        w_sum[:, cols:],
        f_dq.reshape(full_query.shape),
        f_dk_out,
        f_dv_out,
    )


def solution(mesh):
    placed = (
        P(("groups", "seq")),
        P(("groups", "seq"), "head", "rep"),
        P(("groups", "seq"), "head"),
        P(("groups", "seq"), "head"),
        P(("groups", "seq"), "head", "rep"),
        P("head", "rep"),
        P(("groups", "seq"), "head", "rep"),
        P(("groups", "seq"), "head"),
        P(("groups", "seq"), "head"),
        P(("groups", "seq"), "head", "rep"),
        P("head", "rep"),
    )
    return jax.shard_map(
        body,
        mesh=mesh,
        in_specs=placed,
        out_specs=(
            P(("groups", "seq"), "head", "rep"),
            P(("groups", "seq"), "head"),
            P(("groups", "seq"), "head"),
            P(("groups", "seq"), "head", "rep"),
            P(("groups", "seq"), "head"),
            P(("groups", "seq"), "head"),
        ),
        check_vma=False,
    )
```

```python
import functools
import math

import jax
import jax.numpy as jnp
from jax import lax
from jax.experimental import pallas as pl
from jax.experimental.pallas import tpu as pltpu
from jax.sharding import PartitionSpec as P

HD = 64
WINDOW = 128
NEG = -1e30
NT_DIMS = (((1,), (1,)), ((), ()))


def passed_along(value, axis, steps):
    count = lax.axis_size(axis)
    first, last = (max(0, -steps), min(count, count - steps))
    return lax.ppermute(value, axis, [(source, source + steps) for source in range(first, last)])


def pick_half(block, half):
    return jnp.where(half == 0, block[:, :HD], block[:, HD:])


def attn_bwd_kernel(g0, gn, band, sink_ref, q_ref, do_ref, k_ref, v_ref, bias_ref, dq_ref, dk_ref, dv_ref):
    g_rel = pl.program_id(0)
    g = g_rel + g0
    i = pl.program_id(1)
    heads = q_ref.shape[1] // HD

    @pl.when((g_rel == 0) & (i == 0))
    def _():
        dk_ref[...] = jnp.zeros_like(dk_ref)
        dv_ref[...] = jnp.zeros_like(dv_ref)

    k = pick_half(k_ref[...], g % 2)
    v = pick_half(v_ref[...], g % 2)
    bias = bias_ref[...]
    dk_acc = None
    dv_acc = None
    dq_parts = []
    for j in range(heads):
        q = q_ref[:, j * HD:(j + 1) * HD]
        do = do_ref[:, j * HD:(j + 1) * HD]
        sink = sink_ref[g, j]
        s = lax.dot_general(q, k, NT_DIMS, preferred_element_type=jnp.float32) + bias
        row_max = jnp.maximum(jnp.max(s, axis=1, keepdims=True), sink)
        e = jnp.exp(s - row_max)
        total = jnp.sum(e, axis=1, keepdims=True) + jnp.exp(sink - row_max)
        p = e * (1.0 / total)
        p_low = p.astype(jnp.bfloat16)
        dp = lax.dot_general(do, v, NT_DIMS, preferred_element_type=jnp.float32)
        delta = jnp.sum(p_low.astype(jnp.float32) * dp, axis=1, keepdims=True)
        ds_low = (p * (dp - delta)).astype(jnp.bfloat16)
        dq_parts.append(
            (jnp.dot(ds_low, k, preferred_element_type=jnp.float32) * 0.125).astype(dq_ref.dtype)
        )
        dk = jnp.dot(ds_low.T, q, preferred_element_type=jnp.float32)
        dv = jnp.dot(p_low.T, do, preferred_element_type=jnp.float32)
        dk_acc = dk if dk_acc is None else dk_acc + dk
        dv_acc = dv if dv_acc is None else dv_acc + dv
    dq_ref[...] = jnp.concatenate(dq_parts, axis=1)

    key_rows = k.shape[0]
    if band:
        key_span = pl.ds(pl.multiple_of(i * band, band), key_rows)
    else:
        key_span = slice(None)
    for gg in range(gn):
        @pl.when(g_rel == gg)
        def _():
            dk_ref[key_span, gg * HD:(gg + 1) * HD] += dk_acc
            dv_ref[key_span, gg * HD:(gg + 1) * HD] += dv_acc


def attn_bwd(sinks, queries, grads, keys, values, bias, g0, gn, band=None):
    n = queries.shape[0]
    m = keys.shape[0]
    heads = sinks.shape[1]
    rows = n
    while rows > 8 and rows * m > (1 << 18):
        rows //= 2
    width = heads * HD
    if band:
        rows = band
        span = 2 * band
        key_spec = pl.BlockSpec(
            (pl.Element(span), pl.Element(2 * HD)),
            lambda g, i: (i * band, ((g + g0) // 2) * 2 * HD),
        )
        bias_spec = pl.BlockSpec(
            (pl.Element(band), pl.Element(span)), lambda g, i: (i * band, i * band)
        )
    else:
        span = m
        key_spec = pl.BlockSpec((m, 2 * HD), lambda g, i: (0, (g + g0) // 2))
        bias_spec = pl.BlockSpec((rows, m), lambda g, i: (i, 0))
    grid = (gn, n // rows)

    return pl.pallas_call(
        functools.partial(attn_bwd_kernel, g0, gn, band),
        grid=grid,
        in_specs=[
            pl.BlockSpec(memory_space=pltpu.SMEM),
            pl.BlockSpec((rows, width), lambda g, i: (i, g + g0)),
            pl.BlockSpec((rows, width), lambda g, i: (i, g + g0)),
            key_spec,
            key_spec,
            bias_spec,
        ],
        out_specs=[
            pl.BlockSpec((rows, width), lambda g, i: (i, g)),
            pl.BlockSpec((m, gn * HD), lambda g, i: (0, 0)),
            pl.BlockSpec((m, gn * HD), lambda g, i: (0, 0)),
        ],
        out_shape=[
            jax.ShapeDtypeStruct((n, gn * width), jnp.bfloat16),
            jax.ShapeDtypeStruct((m, gn * HD), jnp.float32),
            jax.ShapeDtypeStruct((m, gn * HD), jnp.float32),
        ],
        compiler_params=pltpu.CompilerParams(
            dimension_semantics=("arbitrary", "arbitrary"),
            vmem_limit_bytes=60 * 1024 * 1024,
        ),
        cost_estimate=pl.CostEstimate(
            flops=10 * gn * heads * n * span * HD,
            transcendentals=gn * heads * n * span,
            bytes_accessed=4 * n * span + 4 * n * gn * heads * HD * 3 + 12 * m * gn * HD,
        ),
    )(sinks, queries, grads, keys, values, bias)


def make_bias(query_pos, query_seg, key_pos, key_seg, window):
    distance = query_pos[:, None] - key_pos[None, :]
    visible = (distance >= 0) & (key_pos[None, :] >= 0) & (query_seg[:, None] == key_seg[None, :])
    if window is not None:
        visible = visible & (distance < window)
    return jnp.where(visible, 0.0, NEG).astype(jnp.float32)


def seg_rows(ids, width):
    count = ids.shape[0]
    lines = -(-count // width)
    flat = jnp.zeros((16 * (-(-lines // 16)) * width,), jnp.bfloat16)
    flat = flat.at[:count].set(ids.astype(jnp.bfloat16))
    return flat.reshape(-1, width)


def read_seg(block, count):
    return block.reshape(-1)[:count].astype(jnp.float32).astype(jnp.int32)


def body(
    segment_ids,
    window_query,
    window_keys,
    window_values,
    window_grad_out,
    window_sinks,
    full_query,
    full_keys,
    full_values,
    full_grad_out,
    full_sinks,
):
    n = window_query.shape[0]
    cols = window_keys.shape[1]
    groups = cols // HD
    seq_count = lax.axis_size("seq")
    seq_index = lax.axis_index("seq")
    rep_index = lax.axis_index("rep")
    first = rep_index == 0
    query_pos = seq_index * n + jnp.arange(n)
    order = list(range(seq_count - 1, 0, -1))
    swap = [(0, 1), (1, 0)]

    halo_in = jnp.concatenate(
        [
            jnp.concatenate([window_keys[n - WINDOW:], window_values[n - WINDOW:]], axis=1),
            seg_rows(segment_ids[n - WINDOW:], 2 * cols),
        ],
        axis=0,
    )
    halo = passed_along(halo_in, "seq", 1)

    own_half = jnp.where(first, full_keys, full_values)
    seg_block = seg_rows(segment_ids, cols)
    payload = jnp.concatenate([own_half, seg_block], axis=0)
    halo, payload = lax.optimization_barrier((halo, payload))
    arrived = [passed_along(payload, "seq", d) for d in order]

    w_keys = jnp.concatenate([halo[:WINDOW, :cols], window_keys], axis=0)
    w_values = jnp.concatenate([halo[:WINDOW, cols:], window_values], axis=0)
    w_seg = jnp.concatenate([read_seg(halo[WINDOW:], WINDOW), segment_ids], axis=0)
    w_pos = seq_index * n - WINDOW + jnp.arange(n + WINDOW)
    w_bias = make_bias(query_pos, segment_ids, w_pos, w_seg, WINDOW)
    w_q = (window_query.reshape(n, -1) * 0.125).astype(jnp.bfloat16)
    w_do = window_grad_out.reshape(n, -1)
    g_split = groups // 2 if groups > 1 else groups
    w_band = WINDOW if n % WINDOW == 0 else None
    w_out1 = attn_bwd(window_sinks, w_q, w_do, w_keys, w_values, w_bias, 0, g_split, w_band)

    w_out1, arrived = lax.optimization_barrier((w_out1, arrived))
    mine = jnp.concatenate(arrived, axis=0)
    other = lax.ppermute(mine, "rep", swap)
    step = n + seg_block.shape[0]
    key_parts, value_parts, seg_parts = [], [], []
    for idx in range(len(order)):
        a = mine[idx * step:(idx + 1) * step]
        b = other[idx * step:(idx + 1) * step]
        key_parts.append(jnp.where(first, a[:n], b[:n]))
        value_parts.append(jnp.where(first, b[:n], a[:n]))
        seg_parts.append(read_seg(a[n:], n))
    f_keys = jnp.concatenate(key_parts + [full_keys], axis=0)
    f_values = jnp.concatenate(value_parts + [full_values], axis=0)
    f_seg = jnp.concatenate(seg_parts + [segment_ids], axis=0)
    f_pos = (seq_index - (seq_count - 1)) * n + jnp.arange(seq_count * n)
    f_bias = make_bias(query_pos, segment_ids, f_pos, f_seg, None)
    f_q = (full_query.reshape(n, -1) * 0.125).astype(jnp.bfloat16)
    f_do = full_grad_out.reshape(n, -1)
    f_dq, f_dk, f_dv = attn_bwd(full_sinks, f_q, f_do, f_keys, f_values, f_bias, 0, groups)

    give = jnp.where(first, f_dv, f_dk)
    keep = jnp.where(first, f_dk, f_dv)
    summed = keep + lax.ppermute(give, "rep", swap)
    f_final = summed[(seq_count - 1) * n:]
    for jj, d in enumerate(order):
        piece = summed[jj * n:(jj + 1) * n].astype(jnp.bfloat16)
        f_final = f_final + passed_along(piece, "seq", -d).astype(jnp.float32)

    if g_split < groups:
        w_out2 = attn_bwd(
            window_sinks, w_q, w_do, w_keys, w_values, w_bias, g_split, groups - g_split, w_band
        )
        w_dq = jnp.concatenate([w_out1[0], w_out2[0]], axis=1)
        w_dk = jnp.concatenate([w_out1[1], w_out2[1]], axis=1)
        w_dv = jnp.concatenate([w_out1[2], w_out2[2]], axis=1)
    else:
        w_dq, w_dk, w_dv = w_out1
    back_w = passed_along(
        jnp.concatenate([w_dk[:WINDOW], w_dv[:WINDOW]], axis=1).astype(jnp.bfloat16), "seq", -1
    ).astype(jnp.float32)
    w_kv = jnp.concatenate([w_dk[WINDOW:], w_dv[WINDOW:]], axis=1)
    w_kv = jnp.concatenate([w_kv[: n - WINDOW], w_kv[n - WINDOW:] + back_w], axis=0)

    both = jnp.concatenate([w_kv, f_final], axis=1)
    peer = lax.ppermute(both, "rep", swap)
    w_sum = (w_kv + peer[:, :2 * cols]).astype(jnp.bfloat16)
    f_other = peer[:, 2 * cols:]
    f_dk_out = jnp.where(first, f_final, f_other).astype(jnp.bfloat16)
    f_dv_out = jnp.where(first, f_other, f_final).astype(jnp.bfloat16)
    return (
        w_dq.reshape(window_query.shape),
        w_sum[:, :cols],
        w_sum[:, cols:],
        f_dq.reshape(full_query.shape),
        f_dk_out,
        f_dv_out,
    )


def solution(mesh):
    placed = (
        P(("groups", "seq")),
        P(("groups", "seq"), "head", "rep"),
        P(("groups", "seq"), "head"),
        P(("groups", "seq"), "head"),
        P(("groups", "seq"), "head", "rep"),
        P("head", "rep"),
        P(("groups", "seq"), "head", "rep"),
        P(("groups", "seq"), "head"),
        P(("groups", "seq"), "head"),
        P(("groups", "seq"), "head", "rep"),
        P("head", "rep"),
    )
    return jax.shard_map(
        body,
        mesh=mesh,
        in_specs=placed,
        out_specs=(
            P(("groups", "seq"), "head", "rep"),
            P(("groups", "seq"), "head"),
            P(("groups", "seq"), "head"),
            P(("groups", "seq"), "head", "rep"),
            P(("groups", "seq"), "head"),
            P(("groups", "seq"), "head"),
        ),
        check_vma=False,
    )
```

```python
import functools
import math

import jax
import jax.numpy as jnp
from jax import lax
from jax.experimental import pallas as pl
from jax.experimental.pallas import tpu as pltpu
from jax.sharding import PartitionSpec as P

HD = 64
WINDOW = 128
NEG = -1e30
NT_DIMS = (((1,), (1,)), ((), ()))


def passed_along(value, axis, steps):
    count = lax.axis_size(axis)
    first, last = (max(0, -steps), min(count, count - steps))
    return lax.ppermute(value, axis, [(source, source + steps) for source in range(first, last)])


def pick_half(block, half):
    return jnp.where(half == 0, block[:, :HD], block[:, HD:])


def attn_bwd_kernel(
    g0, gn, window, sink_ref, q_ref, do_ref, k_ref, v_ref, qpos_ref, qseg_ref, kpos_ref, kseg_ref,
    dq_ref, dk_ref, dv_ref,
):
    g_rel = pl.program_id(0)
    g = g_rel + g0
    i = pl.program_id(1)
    heads = q_ref.shape[1] // HD

    @pl.when((g_rel == 0) & (i == 0))
    def _():
        dk_ref[...] = jnp.zeros_like(dk_ref)
        dv_ref[...] = jnp.zeros_like(dv_ref)

    k = pick_half(k_ref[...], g % 2)
    v = pick_half(v_ref[...], g % 2)
    key_pos = kpos_ref[...]
    distance = qpos_ref[...] - key_pos
    visible = (distance >= 0) & (key_pos >= 0) & (qseg_ref[...] == kseg_ref[...])
    if window is not None:
        visible = visible & (distance < window)
    bias = jnp.where(visible, 0.0, NEG).astype(jnp.float32)
    dk_acc = None
    dv_acc = None
    dq_parts = []
    for j in range(heads):
        q = q_ref[:, j * HD:(j + 1) * HD]
        do = do_ref[:, j * HD:(j + 1) * HD]
        sink = sink_ref[g, j]
        s = lax.dot_general(q, k, NT_DIMS, preferred_element_type=jnp.float32) + bias
        row_max = jnp.maximum(jnp.max(s, axis=1, keepdims=True), sink)
        e = jnp.exp(s - row_max)
        total = jnp.sum(e, axis=1, keepdims=True) + jnp.exp(sink - row_max)
        p = e * (1.0 / total)
        p_low = p.astype(jnp.bfloat16)
        dp = lax.dot_general(do, v, NT_DIMS, preferred_element_type=jnp.float32)
        delta = jnp.sum(p_low.astype(jnp.float32) * dp, axis=1, keepdims=True)
        ds_low = (p * (dp - delta)).astype(jnp.bfloat16)
        dq_parts.append(
            (jnp.dot(ds_low, k, preferred_element_type=jnp.float32) * 0.125).astype(dq_ref.dtype)
        )
        dk = jnp.dot(ds_low.T, q, preferred_element_type=jnp.float32)
        dv = jnp.dot(p_low.T, do, preferred_element_type=jnp.float32)
        dk_acc = dk if dk_acc is None else dk_acc + dk
        dv_acc = dv if dv_acc is None else dv_acc + dv
    dq_ref[...] = jnp.concatenate(dq_parts, axis=1)

    for gg in range(gn):
        @pl.when(g_rel == gg)
        def _():
            dk_ref[:, gg * HD:(gg + 1) * HD] += dk_acc
            dv_ref[:, gg * HD:(gg + 1) * HD] += dv_acc


def attn_bwd(sinks, queries, grads, keys, values, mask_info, g0, gn):
    query_pos, query_seg, key_pos, key_seg, window = mask_info
    n = queries.shape[0]
    m = keys.shape[0]
    heads = sinks.shape[1]
    rows = n
    while rows > 8 and rows * m > (1 << 18):
        rows //= 2
    grid = (gn, n // rows)
    width = heads * HD

    return pl.pallas_call(
        functools.partial(attn_bwd_kernel, g0, gn, window),
        grid=grid,
        in_specs=[
            pl.BlockSpec(memory_space=pltpu.SMEM),
            pl.BlockSpec((rows, width), lambda g, i: (i, g + g0)),
            pl.BlockSpec((rows, width), lambda g, i: (i, g + g0)),
            pl.BlockSpec((m, 2 * HD), lambda g, i: (0, (g + g0) // 2)),
            pl.BlockSpec((m, 2 * HD), lambda g, i: (0, (g + g0) // 2)),
            pl.BlockSpec((rows, 1), lambda g, i: (i, 0)),
            pl.BlockSpec((rows, 1), lambda g, i: (i, 0)),
            pl.BlockSpec((1, m), lambda g, i: (0, 0)),
            pl.BlockSpec((1, m), lambda g, i: (0, 0)),
        ],
        out_specs=[
            pl.BlockSpec((rows, width), lambda g, i: (i, g)),
            pl.BlockSpec((m, gn * HD), lambda g, i: (0, 0)),
            pl.BlockSpec((m, gn * HD), lambda g, i: (0, 0)),
        ],
        out_shape=[
            jax.ShapeDtypeStruct((n, gn * width), jnp.bfloat16),
            jax.ShapeDtypeStruct((m, gn * HD), jnp.float32),
            jax.ShapeDtypeStruct((m, gn * HD), jnp.float32),
        ],
        compiler_params=pltpu.CompilerParams(
            dimension_semantics=("arbitrary", "arbitrary"),
            vmem_limit_bytes=60 * 1024 * 1024,
        ),
        cost_estimate=pl.CostEstimate(
            flops=10 * gn * heads * n * m * HD,
            transcendentals=gn * heads * n * m,
            bytes_accessed=8 * (n + m) + 4 * n * gn * heads * HD * 3 + 12 * m * gn * HD,
        ),
    )(
        sinks, queries, grads, keys, values,
        query_pos.reshape(n, 1).astype(jnp.int32), query_seg.reshape(n, 1).astype(jnp.int32),
        key_pos.reshape(1, m).astype(jnp.int32), key_seg.reshape(1, m).astype(jnp.int32),
    )


def make_bias(query_pos, query_seg, key_pos, key_seg, window):
    distance = query_pos[:, None] - key_pos[None, :]
    visible = (distance >= 0) & (key_pos[None, :] >= 0) & (query_seg[:, None] == key_seg[None, :])
    if window is not None:
        visible = visible & (distance < window)
    return jnp.where(visible, 0.0, NEG).astype(jnp.float32)


def seg_rows(ids, width):
    count = ids.shape[0]
    lines = -(-count // width)
    flat = jnp.zeros((16 * (-(-lines // 16)) * width,), jnp.bfloat16)
    flat = flat.at[:count].set(ids.astype(jnp.bfloat16))
    return flat.reshape(-1, width)


def read_seg(block, count):
    return block.reshape(-1)[:count].astype(jnp.float32).astype(jnp.int32)


def body(
    segment_ids,
    window_query,
    window_keys,
    window_values,
    window_grad_out,
    window_sinks,
    full_query,
    full_keys,
    full_values,
    full_grad_out,
    full_sinks,
):
    n = window_query.shape[0]
    cols = window_keys.shape[1]
    groups = cols // HD
    seq_count = lax.axis_size("seq")
    seq_index = lax.axis_index("seq")
    rep_index = lax.axis_index("rep")
    first = rep_index == 0
    query_pos = seq_index * n + jnp.arange(n)
    order = list(range(seq_count - 1, 0, -1))
    swap = [(0, 1), (1, 0)]

    halo_in = jnp.concatenate(
        [
            jnp.concatenate([window_keys[n - WINDOW:], window_values[n - WINDOW:]], axis=1),
            seg_rows(segment_ids[n - WINDOW:], 2 * cols),
        ],
        axis=0,
    )
    halo = passed_along(halo_in, "seq", 1)

    own_half = jnp.where(first, full_keys, full_values)
    seg_block = seg_rows(segment_ids, cols)
    payload = jnp.concatenate([own_half, seg_block], axis=0)
    halo, payload = lax.optimization_barrier((halo, payload))
    arrived = [passed_along(payload, "seq", d) for d in order]

    w_keys = jnp.concatenate([halo[:WINDOW, :cols], window_keys], axis=0)
    w_values = jnp.concatenate([halo[:WINDOW, cols:], window_values], axis=0)
    w_seg = jnp.concatenate([read_seg(halo[WINDOW:], WINDOW), segment_ids], axis=0)
    w_pos = seq_index * n - WINDOW + jnp.arange(n + WINDOW)
    w_bias = (query_pos, segment_ids, w_pos, w_seg, WINDOW)
    w_q = (window_query.reshape(n, -1) * 0.125).astype(jnp.bfloat16)
    w_do = window_grad_out.reshape(n, -1)
    g_split = groups // 2 if groups > 1 else groups
    w_out1 = attn_bwd(window_sinks, w_q, w_do, w_keys, w_values, w_bias, 0, g_split)

    w_out1, arrived = lax.optimization_barrier((w_out1, arrived))
    mine = jnp.concatenate(arrived, axis=0)
    other = lax.ppermute(mine, "rep", swap)
    step = n + seg_block.shape[0]
    key_parts, value_parts, seg_parts = [], [], []
    for idx in range(len(order)):
        a = mine[idx * step:(idx + 1) * step]
        b = other[idx * step:(idx + 1) * step]
        key_parts.append(jnp.where(first, a[:n], b[:n]))
        value_parts.append(jnp.where(first, b[:n], a[:n]))
        seg_parts.append(read_seg(a[n:], n))
    f_keys = jnp.concatenate(key_parts + [full_keys], axis=0)
    f_values = jnp.concatenate(value_parts + [full_values], axis=0)
    f_seg = jnp.concatenate(seg_parts + [segment_ids], axis=0)
    f_pos = (seq_index - (seq_count - 1)) * n + jnp.arange(seq_count * n)
    f_bias = (query_pos, segment_ids, f_pos, f_seg, None)
    f_q = (full_query.reshape(n, -1) * 0.125).astype(jnp.bfloat16)
    f_do = full_grad_out.reshape(n, -1)
    f_dq, f_dk, f_dv = attn_bwd(full_sinks, f_q, f_do, f_keys, f_values, f_bias, 0, groups)

    give = jnp.where(first, f_dv, f_dk)
    keep = jnp.where(first, f_dk, f_dv)
    summed = keep + lax.ppermute(give, "rep", swap)
    f_final = summed[(seq_count - 1) * n:]
    for jj, d in enumerate(order):
        piece = summed[jj * n:(jj + 1) * n].astype(jnp.bfloat16)
        f_final = f_final + passed_along(piece, "seq", -d).astype(jnp.float32)

    if g_split < groups:
        w_out2 = attn_bwd(window_sinks, w_q, w_do, w_keys, w_values, w_bias, g_split, groups - g_split)
        w_dq = jnp.concatenate([w_out1[0], w_out2[0]], axis=1)
        w_dk = jnp.concatenate([w_out1[1], w_out2[1]], axis=1)
        w_dv = jnp.concatenate([w_out1[2], w_out2[2]], axis=1)
    else:
        w_dq, w_dk, w_dv = w_out1
    back_w = passed_along(
        jnp.concatenate([w_dk[:WINDOW], w_dv[:WINDOW]], axis=1).astype(jnp.bfloat16), "seq", -1
    ).astype(jnp.float32)
    w_kv = jnp.concatenate([w_dk[WINDOW:], w_dv[WINDOW:]], axis=1)
    w_kv = jnp.concatenate([w_kv[: n - WINDOW], w_kv[n - WINDOW:] + back_w], axis=0)

    both = jnp.concatenate([w_kv, f_final], axis=1)
    peer = lax.ppermute(both, "rep", swap)
    w_sum = (w_kv + peer[:, :2 * cols]).astype(jnp.bfloat16)
    f_other = peer[:, 2 * cols:]
    f_dk_out = jnp.where(first, f_final, f_other).astype(jnp.bfloat16)
    f_dv_out = jnp.where(first, f_other, f_final).astype(jnp.bfloat16)
    return (
        w_dq.reshape(window_query.shape),
        w_sum[:, :cols],
        w_sum[:, cols:],
        f_dq.reshape(full_query.shape),
        f_dk_out,
        f_dv_out,
    )


def solution(mesh):
    placed = (
        P(("groups", "seq")),
        P(("groups", "seq"), "head", "rep"),
        P(("groups", "seq"), "head"),
        P(("groups", "seq"), "head"),
        P(("groups", "seq"), "head", "rep"),
        P("head", "rep"),
        P(("groups", "seq"), "head", "rep"),
        P(("groups", "seq"), "head"),
        P(("groups", "seq"), "head"),
        P(("groups", "seq"), "head", "rep"),
        P("head", "rep"),
    )
    return jax.shard_map(
        body,
        mesh=mesh,
        in_specs=placed,
        out_specs=(
            P(("groups", "seq"), "head", "rep"),
            P(("groups", "seq"), "head"),
            P(("groups", "seq"), "head"),
            P(("groups", "seq"), "head", "rep"),
            P(("groups", "seq"), "head"),
            P(("groups", "seq"), "head"),
        ),
        check_vma=False,
    )
```

```python
import functools
import math

import jax
import jax.numpy as jnp
from jax import lax
from jax.experimental import pallas as pl
from jax.experimental.pallas import tpu as pltpu
from jax.sharding import PartitionSpec as P

HD = 64
WINDOW = 128
NEG = -1e30
NT_DIMS = (((1,), (1,)), ((), ()))


def passed_along(value, axis, steps):
    count = lax.axis_size(axis)
    first, last = (max(0, -steps), min(count, count - steps))
    return lax.ppermute(value, axis, [(source, source + steps) for source in range(first, last)])


def pick_half(block, half):
    return jnp.where(half == 0, block[:, :HD], block[:, HD:])


def attn_bwd_kernel(g0, gn, sink_ref, q_ref, do_ref, k_ref, v_ref, bias_ref, dq_ref, dk_ref, dv_ref):
    g_rel = pl.program_id(0)
    g = g_rel + g0
    i = pl.program_id(1)
    heads = q_ref.shape[1] // HD

    @pl.when((g_rel == 0) & (i == 0))
    def _():
        dk_ref[...] = jnp.zeros_like(dk_ref)
        dv_ref[...] = jnp.zeros_like(dv_ref)

    k = pick_half(k_ref[...], g % 2)
    v = pick_half(v_ref[...], g % 2)
    bias = bias_ref[...]
    dk_acc = None
    dv_acc = None
    dq_parts = []
    for j in range(heads):
        q = q_ref[:, j * HD:(j + 1) * HD]
        do = do_ref[:, j * HD:(j + 1) * HD]
        sink = sink_ref[g, j]
        s = lax.dot_general(q, k, NT_DIMS, preferred_element_type=jnp.float32) + bias
        row_max = jnp.maximum(jnp.max(s, axis=1, keepdims=True), sink)
        e = jnp.exp(s - row_max)
        total = jnp.sum(e, axis=1, keepdims=True) + jnp.exp(sink - row_max)
        p = e * (1.0 / total)
        p_low = p.astype(jnp.bfloat16)
        dp = lax.dot_general(do, v, NT_DIMS, preferred_element_type=jnp.float32)
        delta = jnp.sum(p_low.astype(jnp.float32) * dp, axis=1, keepdims=True)
        ds_low = (p * (dp - delta)).astype(jnp.bfloat16)
        dq_parts.append(
            (jnp.dot(ds_low, k, preferred_element_type=jnp.float32) * 0.125).astype(dq_ref.dtype)
        )
        dk = jnp.dot(ds_low.T, q, preferred_element_type=jnp.float32)
        dv = jnp.dot(p_low.T, do, preferred_element_type=jnp.float32)
        dk_acc = dk if dk_acc is None else dk_acc + dk
        dv_acc = dv if dv_acc is None else dv_acc + dv
    dq_ref[...] = jnp.concatenate(dq_parts, axis=1)

    for gg in range(gn):
        @pl.when(g_rel == gg)
        def _():
            dk_ref[:, gg * HD:(gg + 1) * HD] += dk_acc
            dv_ref[:, gg * HD:(gg + 1) * HD] += dv_acc


def attn_bwd(sinks, queries, grads, keys, values, bias, g0, gn):
    n = queries.shape[0]
    m = keys.shape[0]
    heads = sinks.shape[1]
    rows = n
    while rows > 8 and rows * m > (1 << 18):
        rows //= 2
    grid = (gn, n // rows)
    width = heads * HD

    return pl.pallas_call(
        functools.partial(attn_bwd_kernel, g0, gn),
        grid=grid,
        in_specs=[
            pl.BlockSpec(memory_space=pltpu.SMEM),
            pl.BlockSpec((rows, width), lambda g, i: (i, g + g0)),
            pl.BlockSpec((rows, width), lambda g, i: (i, g + g0)),
            pl.BlockSpec((m, 2 * HD), lambda g, i: (0, (g + g0) // 2)),
            pl.BlockSpec((m, 2 * HD), lambda g, i: (0, (g + g0) // 2)),
            pl.BlockSpec((rows, m), lambda g, i: (i, 0)),
        ],
        out_specs=[
            pl.BlockSpec((rows, width), lambda g, i: (i, g)),
            pl.BlockSpec((m, gn * HD), lambda g, i: (0, 0)),
            pl.BlockSpec((m, gn * HD), lambda g, i: (0, 0)),
        ],
        out_shape=[
            jax.ShapeDtypeStruct((n, gn * width), jnp.bfloat16),
            jax.ShapeDtypeStruct((m, gn * HD), jnp.float32),
            jax.ShapeDtypeStruct((m, gn * HD), jnp.float32),
        ],
        compiler_params=pltpu.CompilerParams(
            dimension_semantics=("arbitrary", "arbitrary"),
            vmem_limit_bytes=60 * 1024 * 1024,
        ),
        cost_estimate=pl.CostEstimate(
            flops=10 * gn * heads * n * m * HD,
            transcendentals=gn * heads * n * m,
            bytes_accessed=4 * n * m + 4 * n * gn * heads * HD * 3 + 12 * m * gn * HD,
        ),
    )(sinks, queries, grads, keys, values, bias)


def make_bias(query_pos, query_seg, key_pos, key_seg, window):
    distance = query_pos[:, None] - key_pos[None, :]
    visible = (distance >= 0) & (key_pos[None, :] >= 0) & (query_seg[:, None] == key_seg[None, :])
    if window is not None:
        visible = visible & (distance < window)
    return jnp.where(visible, 0.0, NEG).astype(jnp.float32)


def seg_rows(ids, width):
    count = ids.shape[0]
    lines = -(-count // width)
    flat = jnp.zeros((16 * (-(-lines // 16)) * width,), jnp.bfloat16)
    flat = flat.at[:count].set(ids.astype(jnp.bfloat16))
    return flat.reshape(-1, width)


def read_seg(block, count):
    return block.reshape(-1)[:count].astype(jnp.float32).astype(jnp.int32)


def body(
    segment_ids,
    window_query,
    window_keys,
    window_values,
    window_grad_out,
    window_sinks,
    full_query,
    full_keys,
    full_values,
    full_grad_out,
    full_sinks,
):
    n = window_query.shape[0]
    cols = window_keys.shape[1]
    groups = cols // HD
    seq_count = lax.axis_size("seq")
    seq_index = lax.axis_index("seq")
    rep_index = lax.axis_index("rep")
    first = rep_index == 0
    query_pos = seq_index * n + jnp.arange(n)
    order = list(range(seq_count - 1, 0, -1))
    swap = [(0, 1), (1, 0)]

    halo_in = jnp.concatenate(
        [
            jnp.concatenate([window_keys[n - WINDOW:], window_values[n - WINDOW:]], axis=1),
            seg_rows(segment_ids[n - WINDOW:], 2 * cols),
        ],
        axis=0,
    )
    halo = passed_along(halo_in, "seq", 1)

    own_half = jnp.where(first, full_keys, full_values)
    seg_block = seg_rows(segment_ids, cols)
    payload = jnp.concatenate([own_half, seg_block], axis=0)
    halo, payload = lax.optimization_barrier((halo, payload))
    arrived = [passed_along(payload, "seq", d) for d in order]

    w_keys = jnp.concatenate([halo[:WINDOW, :cols], window_keys], axis=0)
    w_values = jnp.concatenate([halo[:WINDOW, cols:], window_values], axis=0)
    w_seg = jnp.concatenate([read_seg(halo[WINDOW:], WINDOW), segment_ids], axis=0)
    w_pos = seq_index * n - WINDOW + jnp.arange(n + WINDOW)
    w_bias = make_bias(query_pos, segment_ids, w_pos, w_seg, WINDOW)
    w_q = (window_query.reshape(n, -1) * 0.125).astype(jnp.bfloat16)
    w_do = window_grad_out.reshape(n, -1)
    g_split = groups // 2 if groups > 1 else groups
    w_out1 = attn_bwd(window_sinks, w_q, w_do, w_keys, w_values, w_bias, 0, g_split)

    w_out1, arrived = lax.optimization_barrier((w_out1, arrived))
    mine = jnp.concatenate(arrived, axis=0)
    other = lax.ppermute(mine, "rep", swap)
    step = n + seg_block.shape[0]
    key_parts, value_parts, seg_parts = [], [], []
    for idx in range(len(order)):
        a = mine[idx * step:(idx + 1) * step]
        b = other[idx * step:(idx + 1) * step]
        key_parts.append(jnp.where(first, a[:n], b[:n]))
        value_parts.append(jnp.where(first, b[:n], a[:n]))
        seg_parts.append(read_seg(a[n:], n))
    f_keys = jnp.concatenate(key_parts + [full_keys], axis=0)
    f_values = jnp.concatenate(value_parts + [full_values], axis=0)
    f_seg = jnp.concatenate(seg_parts + [segment_ids], axis=0)
    f_pos = (seq_index - (seq_count - 1)) * n + jnp.arange(seq_count * n)
    f_bias = make_bias(query_pos, segment_ids, f_pos, f_seg, None)
    f_q = (full_query.reshape(n, -1) * 0.125).astype(jnp.bfloat16)
    f_do = full_grad_out.reshape(n, -1)
    f_dq, f_dk, f_dv = attn_bwd(full_sinks, f_q, f_do, f_keys, f_values, f_bias, 0, groups)

    give = jnp.where(first, f_dv, f_dk)
    keep = jnp.where(first, f_dk, f_dv)
    summed = keep + lax.ppermute(give, "rep", swap)
    if g_split < groups:
        w_out2 = attn_bwd(window_sinks, w_q, w_do, w_keys, w_values, w_bias, g_split, groups - g_split)
        w_dq = jnp.concatenate([w_out1[0], w_out2[0]], axis=1)
        w_dk = jnp.concatenate([w_out1[1], w_out2[1]], axis=1)
        w_dv = jnp.concatenate([w_out1[2], w_out2[2]], axis=1)
    else:
        w_dq, w_dk, w_dv = w_out1

    f_final = summed[(seq_count - 1) * n:]
    back_w = jnp.zeros((WINDOW, 2 * cols), jnp.float32)
    for jj, d in enumerate(order):
        piece = summed[jj * n:(jj + 1) * n]
        if d == 1:
            piece = jnp.concatenate([piece, w_dk[:WINDOW], w_dv[:WINDOW]], axis=0)
        got = passed_along(piece.astype(jnp.bfloat16), "seq", -d).astype(jnp.float32)
        if d == 1:
            back_w = jnp.concatenate([got[n:n + WINDOW], got[n + WINDOW:]], axis=1)
            got = got[:n]
        f_final = f_final + got
    w_kv = jnp.concatenate([w_dk[WINDOW:], w_dv[WINDOW:]], axis=1)
    w_kv = jnp.concatenate([w_kv[: n - WINDOW], w_kv[n - WINDOW:] + back_w], axis=0)

    both = jnp.concatenate([w_kv, f_final], axis=1)
    peer = lax.ppermute(both, "rep", swap)
    w_sum = (w_kv + peer[:, :2 * cols]).astype(jnp.bfloat16)
    f_other = peer[:, 2 * cols:]
    f_dk_out = jnp.where(first, f_final, f_other).astype(jnp.bfloat16)
    f_dv_out = jnp.where(first, f_other, f_final).astype(jnp.bfloat16)
    return (
        w_dq.reshape(window_query.shape),
        w_sum[:, :cols],
        w_sum[:, cols:],
        f_dq.reshape(full_query.shape),
        f_dk_out,
        f_dv_out,
    )


def solution(mesh):
    placed = (
        P(("groups", "seq")),
        P(("groups", "seq"), "head", "rep"),
        P(("groups", "seq"), "head"),
        P(("groups", "seq"), "head"),
        P(("groups", "seq"), "head", "rep"),
        P("head", "rep"),
        P(("groups", "seq"), "head", "rep"),
        P(("groups", "seq"), "head"),
        P(("groups", "seq"), "head"),
        P(("groups", "seq"), "head", "rep"),
        P("head", "rep"),
    )
    return jax.shard_map(
        body,
        mesh=mesh,
        in_specs=placed,
        out_specs=(
            P(("groups", "seq"), "head", "rep"),
            P(("groups", "seq"), "head"),
            P(("groups", "seq"), "head"),
            P(("groups", "seq"), "head", "rep"),
            P(("groups", "seq"), "head"),
            P(("groups", "seq"), "head"),
        ),
        check_vma=False,
    )
```

```python
import functools
import math

import jax
import jax.numpy as jnp
from jax import lax
from jax.experimental import pallas as pl
from jax.experimental.pallas import tpu as pltpu
from jax.sharding import PartitionSpec as P

HD = 64
WINDOW = 128
NEG = -1e30
NT_DIMS = (((1,), (1,)), ((), ()))


def passed_along(value, axis, steps):
    count = lax.axis_size(axis)
    first, last = (max(0, -steps), min(count, count - steps))
    return lax.ppermute(value, axis, [(source, source + steps) for source in range(first, last)])


def pick_half(block, half):
    return jnp.where(half == 0, block[:, :HD], block[:, HD:])


def attn_bwd_kernel(g0, gn, pair, sink_ref, q_ref, do_ref, k_ref, v_ref, bias_ref, dq_ref, dk_ref, dv_ref):
    t = pl.program_id(0)
    i = pl.program_id(1)
    heads = q_ref.shape[1] // (HD * pair)

    @pl.when((t == 0) & (i == 0))
    def _():
        dk_ref[...] = jnp.zeros_like(dk_ref)
        dv_ref[...] = jnp.zeros_like(dv_ref)

    bias = bias_ref[...]
    k_block = k_ref[...]
    v_block = v_ref[...]
    dq_parts = []
    dk_parts = []
    dv_parts = []
    for h in range(pair):
        g = g0 + t * pair + h
        if pair == 2:
            k = k_block[:, h * HD:(h + 1) * HD]
            v = v_block[:, h * HD:(h + 1) * HD]
        else:
            k = pick_half(k_block, g % 2)
            v = pick_half(v_block, g % 2)
        dk_acc = None
        dv_acc = None
        for j in range(heads):
            col = (h * heads + j) * HD
            q = q_ref[:, col:col + HD]
            do = do_ref[:, col:col + HD]
            sink = sink_ref[g, j]
            s = lax.dot_general(q, k, NT_DIMS, preferred_element_type=jnp.float32) + bias
            row_max = jnp.maximum(jnp.max(s, axis=1, keepdims=True), sink)
            e = jnp.exp(s - row_max)
            total = jnp.sum(e, axis=1, keepdims=True) + jnp.exp(sink - row_max)
            p = e * (1.0 / total)
            p_low = p.astype(jnp.bfloat16)
            dp = lax.dot_general(do, v, NT_DIMS, preferred_element_type=jnp.float32)
            delta = jnp.sum(p_low.astype(jnp.float32) * dp, axis=1, keepdims=True)
            ds_low = (p * (dp - delta)).astype(jnp.bfloat16)
            dq_parts.append(
                (jnp.dot(ds_low, k, preferred_element_type=jnp.float32) * 0.125).astype(dq_ref.dtype)
            )
            dk = jnp.dot(ds_low.T, q, preferred_element_type=jnp.float32)
            dv = jnp.dot(p_low.T, do, preferred_element_type=jnp.float32)
            dk_acc = dk if dk_acc is None else dk_acc + dk
            dv_acc = dv if dv_acc is None else dv_acc + dv
        dk_parts.append(dk_acc)
        dv_parts.append(dv_acc)
    dq_ref[...] = jnp.concatenate(dq_parts, axis=1)
    dk_step = jnp.concatenate(dk_parts, axis=1) if pair == 2 else dk_parts[0]
    dv_step = jnp.concatenate(dv_parts, axis=1) if pair == 2 else dv_parts[0]
    wide = pair * HD

    for tt in range(gn // pair):
        @pl.when(t == tt)
        def _():
            dk_ref[:, tt * wide:(tt + 1) * wide] += dk_step
            dv_ref[:, tt * wide:(tt + 1) * wide] += dv_step


def attn_bwd(sinks, queries, grads, keys, values, bias, g0, gn):
    n = queries.shape[0]
    m = keys.shape[0]
    heads = sinks.shape[1]
    pair = 2 if (g0 % 2 == 0 and gn % 2 == 0) else 1
    rows = n
    while rows > 8 and rows * m > (1 << 18):
        rows //= 2
    grid = (gn // pair, n // rows)
    width = heads * HD * pair
    if pair == 2:
        key_map = lambda t, i: (0, g0 // 2 + t)
    else:
        key_map = lambda t, i: (0, (g0 + t) // 2)

    return pl.pallas_call(
        functools.partial(attn_bwd_kernel, g0, gn, pair),
        grid=grid,
        in_specs=[
            pl.BlockSpec(memory_space=pltpu.SMEM),
            pl.BlockSpec((rows, width), lambda t, i: (i, g0 // pair + t)),
            pl.BlockSpec((rows, width), lambda t, i: (i, g0 // pair + t)),
            pl.BlockSpec((m, 2 * HD), key_map),
            pl.BlockSpec((m, 2 * HD), key_map),
            pl.BlockSpec((rows, m), lambda t, i: (i, 0)),
        ],
        out_specs=[
            pl.BlockSpec((rows, width), lambda t, i: (i, t)),
            pl.BlockSpec((m, gn * HD), lambda t, i: (0, 0)),
            pl.BlockSpec((m, gn * HD), lambda t, i: (0, 0)),
        ],
        out_shape=[
            jax.ShapeDtypeStruct((n, gn * heads * HD), jnp.bfloat16),
            jax.ShapeDtypeStruct((m, gn * HD), jnp.float32),
            jax.ShapeDtypeStruct((m, gn * HD), jnp.float32),
        ],
        compiler_params=pltpu.CompilerParams(
            dimension_semantics=("arbitrary", "arbitrary"),
            vmem_limit_bytes=60 * 1024 * 1024,
        ),
        cost_estimate=pl.CostEstimate(
            flops=10 * gn * heads * n * m * HD,
            transcendentals=gn * heads * n * m,
            bytes_accessed=4 * n * m + 4 * n * gn * heads * HD * 3 + 12 * m * gn * HD,
        ),
    )(sinks, queries, grads, keys, values, bias)


def make_bias(query_pos, query_seg, key_pos, key_seg, window):
    distance = query_pos[:, None] - key_pos[None, :]
    visible = (distance >= 0) & (key_pos[None, :] >= 0) & (query_seg[:, None] == key_seg[None, :])
    if window is not None:
        visible = visible & (distance < window)
    return jnp.where(visible, 0.0, NEG).astype(jnp.float32)


def seg_rows(ids, width):
    count = ids.shape[0]
    lines = -(-count // width)
    flat = jnp.zeros((16 * (-(-lines // 16)) * width,), jnp.bfloat16)
    flat = flat.at[:count].set(ids.astype(jnp.bfloat16))
    return flat.reshape(-1, width)


def read_seg(block, count):
    return block.reshape(-1)[:count].astype(jnp.float32).astype(jnp.int32)


def body(
    segment_ids,
    window_query,
    window_keys,
    window_values,
    window_grad_out,
    window_sinks,
    full_query,
    full_keys,
    full_values,
    full_grad_out,
    full_sinks,
):
    n = window_query.shape[0]
    cols = window_keys.shape[1]
    groups = cols // HD
    seq_count = lax.axis_size("seq")
    seq_index = lax.axis_index("seq")
    rep_index = lax.axis_index("rep")
    first = rep_index == 0
    query_pos = seq_index * n + jnp.arange(n)
    order = list(range(seq_count - 1, 0, -1))
    swap = [(0, 1), (1, 0)]

    halo_in = jnp.concatenate(
        [
            jnp.concatenate([window_keys[n - WINDOW:], window_values[n - WINDOW:]], axis=1),
            seg_rows(segment_ids[n - WINDOW:], 2 * cols),
        ],
        axis=0,
    )
    halo = passed_along(halo_in, "seq", 1)

    own_half = jnp.where(first, full_keys, full_values)
    seg_block = seg_rows(segment_ids, cols)
    payload = jnp.concatenate([own_half, seg_block], axis=0)
    halo, payload = lax.optimization_barrier((halo, payload))
    arrived = [passed_along(payload, "seq", d) for d in order]

    w_keys = jnp.concatenate([halo[:WINDOW, :cols], window_keys], axis=0)
    w_values = jnp.concatenate([halo[:WINDOW, cols:], window_values], axis=0)
    w_seg = jnp.concatenate([read_seg(halo[WINDOW:], WINDOW), segment_ids], axis=0)
    w_pos = seq_index * n - WINDOW + jnp.arange(n + WINDOW)
    w_bias = make_bias(query_pos, segment_ids, w_pos, w_seg, WINDOW)
    w_q = (window_query.reshape(n, -1) * 0.125).astype(jnp.bfloat16)
    w_do = window_grad_out.reshape(n, -1)
    g_split = groups // 2 if groups > 1 else groups
    w_out1 = attn_bwd(window_sinks, w_q, w_do, w_keys, w_values, w_bias, 0, g_split)

    w_out1, arrived = lax.optimization_barrier((w_out1, arrived))
    mine = jnp.concatenate(arrived, axis=0)
    other = lax.ppermute(mine, "rep", swap)
    step = n + seg_block.shape[0]
    key_parts, value_parts, seg_parts = [], [], []
    for idx in range(len(order)):
        a = mine[idx * step:(idx + 1) * step]
        b = other[idx * step:(idx + 1) * step]
        key_parts.append(jnp.where(first, a[:n], b[:n]))
        value_parts.append(jnp.where(first, b[:n], a[:n]))
        seg_parts.append(read_seg(a[n:], n))
    f_keys = jnp.concatenate(key_parts + [full_keys], axis=0)
    f_values = jnp.concatenate(value_parts + [full_values], axis=0)
    f_seg = jnp.concatenate(seg_parts + [segment_ids], axis=0)
    f_pos = (seq_index - (seq_count - 1)) * n + jnp.arange(seq_count * n)
    f_bias = make_bias(query_pos, segment_ids, f_pos, f_seg, None)
    f_q = (full_query.reshape(n, -1) * 0.125).astype(jnp.bfloat16)
    f_do = full_grad_out.reshape(n, -1)
    f_dq, f_dk, f_dv = attn_bwd(full_sinks, f_q, f_do, f_keys, f_values, f_bias, 0, groups)

    give = jnp.where(first, f_dv, f_dk)
    keep = jnp.where(first, f_dk, f_dv)
    summed = keep + lax.ppermute(give, "rep", swap)
    if g_split < groups:
        w_out2 = attn_bwd(window_sinks, w_q, w_do, w_keys, w_values, w_bias, g_split, groups - g_split)
        w_dq = jnp.concatenate([w_out1[0], w_out2[0]], axis=1)
        w_dk = jnp.concatenate([w_out1[1], w_out2[1]], axis=1)
        w_dv = jnp.concatenate([w_out1[2], w_out2[2]], axis=1)
    else:
        w_dq, w_dk, w_dv = w_out1

    f_final = summed[(seq_count - 1) * n:]
    back_w = jnp.zeros((WINDOW, 2 * cols), jnp.float32)
    for jj, d in enumerate(order):
        piece = summed[jj * n:(jj + 1) * n]
        if d == 1:
            piece = jnp.concatenate([piece, w_dk[:WINDOW], w_dv[:WINDOW]], axis=0)
        got = passed_along(piece.astype(jnp.bfloat16), "seq", -d).astype(jnp.float32)
        if d == 1:
            back_w = jnp.concatenate([got[n:n + WINDOW], got[n + WINDOW:]], axis=1)
            got = got[:n]
        f_final = f_final + got
    w_kv = jnp.concatenate([w_dk[WINDOW:], w_dv[WINDOW:]], axis=1)
    w_kv = jnp.concatenate([w_kv[: n - WINDOW], w_kv[n - WINDOW:] + back_w], axis=0)

    both = jnp.concatenate([w_kv, f_final], axis=1)
    peer = lax.ppermute(both, "rep", swap)
    w_sum = (w_kv + peer[:, :2 * cols]).astype(jnp.bfloat16)
    f_other = peer[:, 2 * cols:]
    f_dk_out = jnp.where(first, f_final, f_other).astype(jnp.bfloat16)
    f_dv_out = jnp.where(first, f_other, f_final).astype(jnp.bfloat16)
    return (
        w_dq.reshape(window_query.shape),
        w_sum[:, :cols],
        w_sum[:, cols:],
        f_dq.reshape(full_query.shape),
        f_dk_out,
        f_dv_out,
    )


def solution(mesh):
    placed = (
        P(("groups", "seq")),
        P(("groups", "seq"), "head", "rep"),
        P(("groups", "seq"), "head"),
        P(("groups", "seq"), "head"),
        P(("groups", "seq"), "head", "rep"),
        P("head", "rep"),
        P(("groups", "seq"), "head", "rep"),
        P(("groups", "seq"), "head"),
        P(("groups", "seq"), "head"),
        P(("groups", "seq"), "head", "rep"),
        P("head", "rep"),
    )
    return jax.shard_map(
        body,
        mesh=mesh,
        in_specs=placed,
        out_specs=(
            P(("groups", "seq"), "head", "rep"),
            P(("groups", "seq"), "head"),
            P(("groups", "seq"), "head"),
            P(("groups", "seq"), "head", "rep"),
            P(("groups", "seq"), "head"),
            P(("groups", "seq"), "head"),
        ),
        check_vma=False,
    )
```

```python
import functools
import math

import jax
import jax.numpy as jnp
from jax import lax
from jax.experimental import pallas as pl
from jax.experimental.pallas import tpu as pltpu
from jax.sharding import PartitionSpec as P

HD = 64
WINDOW = 128
NEG = -1e30
NT_DIMS = (((1,), (1,)), ((), ()))


def passed_along(value, axis, steps):
    count = lax.axis_size(axis)
    first, last = (max(0, -steps), min(count, count - steps))
    return lax.ppermute(value, axis, [(source, source + steps) for source in range(first, last)])


def pick_half(block, half):
    return jnp.where(half == 0, block[:, :HD], block[:, HD:])


def attn_bwd_kernel(g0, gn, pair, sink_ref, q_ref, do_ref, k_ref, v_ref, bias_ref, dq_ref, dk_ref, dv_ref):
    t = pl.program_id(0)
    i = pl.program_id(1)
    heads = q_ref.shape[1] // (HD * pair)

    @pl.when((t == 0) & (i == 0))
    def _():
        dk_ref[...] = jnp.zeros_like(dk_ref)
        dv_ref[...] = jnp.zeros_like(dv_ref)

    bias = bias_ref[...]
    k_block = k_ref[...]
    v_block = v_ref[...]
    dq_parts = []
    dk_parts = []
    dv_parts = []
    for h in range(pair):
        g = g0 + t * pair + h
        if pair >= 2:
            k = k_block[:, h * HD:(h + 1) * HD]
            v = v_block[:, h * HD:(h + 1) * HD]
        else:
            k = pick_half(k_block, g % 2)
            v = pick_half(v_block, g % 2)
        dk_acc = None
        dv_acc = None
        for j in range(heads):
            col = (h * heads + j) * HD
            q = q_ref[:, col:col + HD]
            do = do_ref[:, col:col + HD]
            sink = sink_ref[g, j]
            s = lax.dot_general(q, k, NT_DIMS, preferred_element_type=jnp.float32) + bias
            row_max = jnp.maximum(jnp.max(s, axis=1, keepdims=True), sink)
            e = jnp.exp(s - row_max)
            total = jnp.sum(e, axis=1, keepdims=True) + jnp.exp(sink - row_max)
            p = e * (1.0 / total)
            p_low = p.astype(jnp.bfloat16)
            dp = lax.dot_general(do, v, NT_DIMS, preferred_element_type=jnp.float32)
            delta = jnp.sum(p_low.astype(jnp.float32) * dp, axis=1, keepdims=True)
            ds_low = (p * (dp - delta)).astype(jnp.bfloat16)
            dq_parts.append(
                (jnp.dot(ds_low, k, preferred_element_type=jnp.float32) * 0.125).astype(dq_ref.dtype)
            )
            dk = jnp.dot(ds_low.T, q, preferred_element_type=jnp.float32)
            dv = jnp.dot(p_low.T, do, preferred_element_type=jnp.float32)
            dk_acc = dk if dk_acc is None else dk_acc + dk
            dv_acc = dv if dv_acc is None else dv_acc + dv
        dk_parts.append(dk_acc)
        dv_parts.append(dv_acc)
    dq_ref[...] = jnp.concatenate(dq_parts, axis=1)
    dk_step = jnp.concatenate(dk_parts, axis=1) if pair >= 2 else dk_parts[0]
    dv_step = jnp.concatenate(dv_parts, axis=1) if pair >= 2 else dv_parts[0]
    wide = pair * HD

    for tt in range(gn // pair):
        @pl.when(t == tt)
        def _():
            dk_ref[:, tt * wide:(tt + 1) * wide] += dk_step
            dv_ref[:, tt * wide:(tt + 1) * wide] += dv_step


def attn_bwd(sinks, queries, grads, keys, values, bias, g0, gn):
    n = queries.shape[0]
    m = keys.shape[0]
    heads = sinks.shape[1]
    if gn % 2 == 0 and g0 % gn == 0:
        pair = gn
    elif gn % 2 == 0 and g0 % 2 == 0:
        pair = 2
    else:
        pair = 1
    rows = n
    while rows > 8 and rows * m > (1 << 18):
        rows //= 2
    grid = (gn // pair, n // rows)
    width = heads * HD * pair
    if pair >= 2:
        key_width = pair * HD
        key_map = lambda t, i: (0, g0 // pair + t)
    else:
        key_width = 2 * HD
        key_map = lambda t, i: (0, (g0 + t) // 2)

    return pl.pallas_call(
        functools.partial(attn_bwd_kernel, g0, gn, pair),
        grid=grid,
        in_specs=[
            pl.BlockSpec(memory_space=pltpu.SMEM),
            pl.BlockSpec((rows, width), lambda t, i: (i, g0 // pair + t)),
            pl.BlockSpec((rows, width), lambda t, i: (i, g0 // pair + t)),
            pl.BlockSpec((m, key_width), key_map),
            pl.BlockSpec((m, key_width), key_map),
            pl.BlockSpec((rows, m), lambda t, i: (i, 0)),
        ],
        out_specs=[
            pl.BlockSpec((rows, width), lambda t, i: (i, t)),
            pl.BlockSpec((m, gn * HD), lambda t, i: (0, 0)),
            pl.BlockSpec((m, gn * HD), lambda t, i: (0, 0)),
        ],
        out_shape=[
            jax.ShapeDtypeStruct((n, gn * heads * HD), jnp.bfloat16),
            jax.ShapeDtypeStruct((m, gn * HD), jnp.float32),
            jax.ShapeDtypeStruct((m, gn * HD), jnp.float32),
        ],
        compiler_params=pltpu.CompilerParams(
            dimension_semantics=("arbitrary", "arbitrary"),
            vmem_limit_bytes=60 * 1024 * 1024,
        ),
        cost_estimate=pl.CostEstimate(
            flops=10 * gn * heads * n * m * HD,
            transcendentals=gn * heads * n * m,
            bytes_accessed=4 * n * m + 4 * n * gn * heads * HD * 3 + 12 * m * gn * HD,
        ),
    )(sinks, queries, grads, keys, values, bias)


def make_bias(query_pos, query_seg, key_pos, key_seg, window):
    distance = query_pos[:, None] - key_pos[None, :]
    visible = (distance >= 0) & (key_pos[None, :] >= 0) & (query_seg[:, None] == key_seg[None, :])
    if window is not None:
        visible = visible & (distance < window)
    return jnp.where(visible, 0.0, NEG).astype(jnp.float32)


def seg_rows(ids, width):
    count = ids.shape[0]
    lines = -(-count // width)
    flat = jnp.zeros((16 * (-(-lines // 16)) * width,), jnp.bfloat16)
    flat = flat.at[:count].set(ids.astype(jnp.bfloat16))
    return flat.reshape(-1, width)


def read_seg(block, count):
    return block.reshape(-1)[:count].astype(jnp.float32).astype(jnp.int32)


def body(
    segment_ids,
    window_query,
    window_keys,
    window_values,
    window_grad_out,
    window_sinks,
    full_query,
    full_keys,
    full_values,
    full_grad_out,
    full_sinks,
):
    n = window_query.shape[0]
    cols = window_keys.shape[1]
    groups = cols // HD
    seq_count = lax.axis_size("seq")
    seq_index = lax.axis_index("seq")
    rep_index = lax.axis_index("rep")
    first = rep_index == 0
    query_pos = seq_index * n + jnp.arange(n)
    order = list(range(seq_count - 1, 0, -1))
    swap = [(0, 1), (1, 0)]

    halo_in = jnp.concatenate(
        [
            jnp.concatenate([window_keys[n - WINDOW:], window_values[n - WINDOW:]], axis=1),
            seg_rows(segment_ids[n - WINDOW:], 2 * cols),
        ],
        axis=0,
    )
    halo = passed_along(halo_in, "seq", 1)

    own_half = jnp.where(first, full_keys, full_values)
    seg_block = seg_rows(segment_ids, cols)
    payload = jnp.concatenate([own_half, seg_block], axis=0)
    halo, payload = lax.optimization_barrier((halo, payload))
    arrived = [passed_along(payload, "seq", d) for d in order]

    w_keys = jnp.concatenate([halo[:WINDOW, :cols], window_keys], axis=0)
    w_values = jnp.concatenate([halo[:WINDOW, cols:], window_values], axis=0)
    w_seg = jnp.concatenate([read_seg(halo[WINDOW:], WINDOW), segment_ids], axis=0)
    w_pos = seq_index * n - WINDOW + jnp.arange(n + WINDOW)
    w_bias = make_bias(query_pos, segment_ids, w_pos, w_seg, WINDOW)
    w_q = (window_query.reshape(n, -1) * 0.125).astype(jnp.bfloat16)
    w_do = window_grad_out.reshape(n, -1)
    g_split = groups // 2 if groups > 1 else groups
    w_out1 = attn_bwd(window_sinks, w_q, w_do, w_keys, w_values, w_bias, 0, g_split)

    w_out1, arrived = lax.optimization_barrier((w_out1, arrived))
    mine = jnp.concatenate(arrived, axis=0)
    other = lax.ppermute(mine, "rep", swap)
    step = n + seg_block.shape[0]
    key_parts, value_parts, seg_parts = [], [], []
    for idx in range(len(order)):
        a = mine[idx * step:(idx + 1) * step]
        b = other[idx * step:(idx + 1) * step]
        key_parts.append(jnp.where(first, a[:n], b[:n]))
        value_parts.append(jnp.where(first, b[:n], a[:n]))
        seg_parts.append(read_seg(a[n:], n))
    f_keys = jnp.concatenate(key_parts + [full_keys], axis=0)
    f_values = jnp.concatenate(value_parts + [full_values], axis=0)
    f_seg = jnp.concatenate(seg_parts + [segment_ids], axis=0)
    f_pos = (seq_index - (seq_count - 1)) * n + jnp.arange(seq_count * n)
    f_bias = make_bias(query_pos, segment_ids, f_pos, f_seg, None)
    f_q = (full_query.reshape(n, -1) * 0.125).astype(jnp.bfloat16)
    f_do = full_grad_out.reshape(n, -1)
    f_dq, f_dk, f_dv = attn_bwd(full_sinks, f_q, f_do, f_keys, f_values, f_bias, 0, groups)

    give = jnp.where(first, f_dv, f_dk)
    keep = jnp.where(first, f_dk, f_dv)
    summed = keep + lax.ppermute(give, "rep", swap)
    if g_split < groups:
        w_out2 = attn_bwd(window_sinks, w_q, w_do, w_keys, w_values, w_bias, g_split, groups - g_split)
        w_dq = jnp.concatenate([w_out1[0], w_out2[0]], axis=1)
        w_dk = jnp.concatenate([w_out1[1], w_out2[1]], axis=1)
        w_dv = jnp.concatenate([w_out1[2], w_out2[2]], axis=1)
    else:
        w_dq, w_dk, w_dv = w_out1

    f_final = summed[(seq_count - 1) * n:]
    back_w = jnp.zeros((WINDOW, 2 * cols), jnp.float32)
    for jj, d in enumerate(order):
        piece = summed[jj * n:(jj + 1) * n]
        if d == 1:
            piece = jnp.concatenate([piece, w_dk[:WINDOW], w_dv[:WINDOW]], axis=0)
        got = passed_along(piece.astype(jnp.bfloat16), "seq", -d).astype(jnp.float32)
        if d == 1:
            back_w = jnp.concatenate([got[n:n + WINDOW], got[n + WINDOW:]], axis=1)
            got = got[:n]
        f_final = f_final + got
    w_kv = jnp.concatenate([w_dk[WINDOW:], w_dv[WINDOW:]], axis=1)
    w_kv = jnp.concatenate([w_kv[: n - WINDOW], w_kv[n - WINDOW:] + back_w], axis=0)

    both = jnp.concatenate([w_kv, f_final], axis=1)
    peer = lax.ppermute(both, "rep", swap)
    w_sum = (w_kv + peer[:, :2 * cols]).astype(jnp.bfloat16)
    f_other = peer[:, 2 * cols:]
    f_dk_out = jnp.where(first, f_final, f_other).astype(jnp.bfloat16)
    f_dv_out = jnp.where(first, f_other, f_final).astype(jnp.bfloat16)
    return (
        w_dq.reshape(window_query.shape),
        w_sum[:, :cols],
        w_sum[:, cols:],
        f_dq.reshape(full_query.shape),
        f_dk_out,
        f_dv_out,
    )


def solution(mesh):
    placed = (
        P(("groups", "seq")),
        P(("groups", "seq"), "head", "rep"),
        P(("groups", "seq"), "head"),
        P(("groups", "seq"), "head"),
        P(("groups", "seq"), "head", "rep"),
        P("head", "rep"),
        P(("groups", "seq"), "head", "rep"),
        P(("groups", "seq"), "head"),
        P(("groups", "seq"), "head"),
        P(("groups", "seq"), "head", "rep"),
        P("head", "rep"),
    )
    return jax.shard_map(
        body,
        mesh=mesh,
        in_specs=placed,
        out_specs=(
            P(("groups", "seq"), "head", "rep"),
            P(("groups", "seq"), "head"),
            P(("groups", "seq"), "head"),
            P(("groups", "seq"), "head", "rep"),
            P(("groups", "seq"), "head"),
            P(("groups", "seq"), "head"),
        ),
        check_vma=False,
    )
```

```python
import functools
import math

import jax
import jax.numpy as jnp
from jax import lax
from jax.experimental import pallas as pl
from jax.experimental.pallas import tpu as pltpu
from jax.sharding import PartitionSpec as P

HD = 64
WINDOW = 128
NEG = -1e30
NT_DIMS = (((1,), (1,)), ((), ()))


def passed_along(value, axis, steps):
    count = lax.axis_size(axis)
    first, last = (max(0, -steps), min(count, count - steps))
    return lax.ppermute(value, axis, [(source, source + steps) for source in range(first, last)])


def pick_half(block, half):
    return jnp.where(half == 0, block[:, :HD], block[:, HD:])


def attn_bwd_kernel(
    g0, gn, pair, window, sink_ref, q_ref, do_ref, k_ref, v_ref, qpos_ref, qseg_ref, kpos_ref, kseg_ref,
    dq_ref, dk_ref, dv_ref,
):
    t = pl.program_id(0)
    i = pl.program_id(1)
    heads = q_ref.shape[1] // (HD * pair)

    @pl.when((t == 0) & (i == 0))
    def _():
        dk_ref[...] = jnp.zeros_like(dk_ref)
        dv_ref[...] = jnp.zeros_like(dv_ref)

    key_pos = kpos_ref[...]
    distance = qpos_ref[...] - key_pos
    visible = (distance >= 0) & (key_pos >= 0) & (qseg_ref[...] == kseg_ref[...])
    if window is not None:
        visible = visible & (distance < window)
    bias = jnp.where(visible, 0.0, NEG).astype(jnp.float32)
    k_block = k_ref[...]
    v_block = v_ref[...]
    dq_parts = []
    dk_parts = []
    dv_parts = []
    for h in range(pair):
        g = g0 + t * pair + h
        if pair >= 2:
            k = k_block[:, h * HD:(h + 1) * HD]
            v = v_block[:, h * HD:(h + 1) * HD]
        else:
            k = pick_half(k_block, g % 2)
            v = pick_half(v_block, g % 2)
        dk_acc = None
        dv_acc = None
        for j in range(heads):
            col = (h * heads + j) * HD
            q = q_ref[:, col:col + HD]
            do = do_ref[:, col:col + HD]
            sink = sink_ref[g, j]
            s = lax.dot_general(q, k, NT_DIMS, preferred_element_type=jnp.float32) + bias
            row_max = jnp.maximum(jnp.max(s, axis=1, keepdims=True), sink)
            e = jnp.exp(s - row_max)
            total = jnp.sum(e, axis=1, keepdims=True) + jnp.exp(sink - row_max)
            p = e * (1.0 / total)
            p_low = p.astype(jnp.bfloat16)
            dp = lax.dot_general(do, v, NT_DIMS, preferred_element_type=jnp.float32)
            delta = jnp.sum(p_low.astype(jnp.float32) * dp, axis=1, keepdims=True)
            ds_low = (p * (dp - delta)).astype(jnp.bfloat16)
            dq_parts.append(
                (jnp.dot(ds_low, k, preferred_element_type=jnp.float32) * 0.125).astype(dq_ref.dtype)
            )
            dk = jnp.dot(ds_low.T, q, preferred_element_type=jnp.float32)
            dv = jnp.dot(p_low.T, do, preferred_element_type=jnp.float32)
            dk_acc = dk if dk_acc is None else dk_acc + dk
            dv_acc = dv if dv_acc is None else dv_acc + dv
        dk_parts.append(dk_acc)
        dv_parts.append(dv_acc)
    dq_ref[...] = jnp.concatenate(dq_parts, axis=1)
    dk_step = jnp.concatenate(dk_parts, axis=1) if pair >= 2 else dk_parts[0]
    dv_step = jnp.concatenate(dv_parts, axis=1) if pair >= 2 else dv_parts[0]
    wide = pair * HD

    for tt in range(gn // pair):
        @pl.when(t == tt)
        def _():
            dk_ref[:, tt * wide:(tt + 1) * wide] += dk_step
            dv_ref[:, tt * wide:(tt + 1) * wide] += dv_step


def attn_bwd(sinks, queries, grads, keys, values, mask_info, g0, gn):
    query_pos, query_seg, key_pos, key_seg, window = mask_info
    n = queries.shape[0]
    m = keys.shape[0]
    heads = sinks.shape[1]
    if gn % 2 == 0 and g0 % gn == 0:
        pair = gn
    elif gn % 2 == 0 and g0 % 2 == 0:
        pair = 2
    else:
        pair = 1
    rows = n
    while rows > 8 and rows * m > (1 << 18):
        rows //= 2
    grid = (gn // pair, n // rows)
    width = heads * HD * pair
    if pair >= 2:
        key_width = pair * HD
        key_map = lambda t, i: (0, g0 // pair + t)
    else:
        key_width = 2 * HD
        key_map = lambda t, i: (0, (g0 + t) // 2)

    return pl.pallas_call(
        functools.partial(attn_bwd_kernel, g0, gn, pair, window),
        grid=grid,
        in_specs=[
            pl.BlockSpec(memory_space=pltpu.SMEM),
            pl.BlockSpec((rows, width), lambda t, i: (i, g0 // pair + t)),
            pl.BlockSpec((rows, width), lambda t, i: (i, g0 // pair + t)),
            pl.BlockSpec((m, key_width), key_map),
            pl.BlockSpec((m, key_width), key_map),
            pl.BlockSpec((rows, 1), lambda t, i: (i, 0)),
            pl.BlockSpec((rows, 1), lambda t, i: (i, 0)),
            pl.BlockSpec((1, m), lambda t, i: (0, 0)),
            pl.BlockSpec((1, m), lambda t, i: (0, 0)),
        ],
        out_specs=[
            pl.BlockSpec((rows, width), lambda t, i: (i, t)),
            pl.BlockSpec((m, gn * HD), lambda t, i: (0, 0)),
            pl.BlockSpec((m, gn * HD), lambda t, i: (0, 0)),
        ],
        out_shape=[
            jax.ShapeDtypeStruct((n, gn * heads * HD), jnp.bfloat16),
            jax.ShapeDtypeStruct((m, gn * HD), jnp.float32),
            jax.ShapeDtypeStruct((m, gn * HD), jnp.float32),
        ],
        compiler_params=pltpu.CompilerParams(
            dimension_semantics=("arbitrary", "arbitrary"),
            vmem_limit_bytes=60 * 1024 * 1024,
        ),
        cost_estimate=pl.CostEstimate(
            flops=10 * gn * heads * n * m * HD,
            transcendentals=gn * heads * n * m,
            bytes_accessed=8 * (n + m) + 4 * n * gn * heads * HD * 3 + 12 * m * gn * HD,
        ),
    )(
        sinks, queries, grads, keys, values,
        query_pos.reshape(n, 1).astype(jnp.int32), query_seg.reshape(n, 1).astype(jnp.int32),
        key_pos.reshape(1, m).astype(jnp.int32), key_seg.reshape(1, m).astype(jnp.int32),
    )


def make_bias(query_pos, query_seg, key_pos, key_seg, window):
    distance = query_pos[:, None] - key_pos[None, :]
    visible = (distance >= 0) & (key_pos[None, :] >= 0) & (query_seg[:, None] == key_seg[None, :])
    if window is not None:
        visible = visible & (distance < window)
    return jnp.where(visible, 0.0, NEG).astype(jnp.float32)


def seg_rows(ids, width):
    count = ids.shape[0]
    lines = -(-count // width)
    flat = jnp.zeros((16 * (-(-lines // 16)) * width,), jnp.bfloat16)
    flat = flat.at[:count].set(ids.astype(jnp.bfloat16))
    return flat.reshape(-1, width)


def read_seg(block, count):
    return block.reshape(-1)[:count].astype(jnp.float32).astype(jnp.int32)


def body(
    segment_ids,
    window_query,
    window_keys,
    window_values,
    window_grad_out,
    window_sinks,
    full_query,
    full_keys,
    full_values,
    full_grad_out,
    full_sinks,
):
    n = window_query.shape[0]
    cols = window_keys.shape[1]
    groups = cols // HD
    seq_count = lax.axis_size("seq")
    seq_index = lax.axis_index("seq")
    rep_index = lax.axis_index("rep")
    first = rep_index == 0
    query_pos = seq_index * n + jnp.arange(n)
    order = list(range(seq_count - 1, 0, -1))
    swap = [(0, 1), (1, 0)]

    halo_in = jnp.concatenate(
        [
            jnp.concatenate([window_keys[n - WINDOW:], window_values[n - WINDOW:]], axis=1),
            seg_rows(segment_ids[n - WINDOW:], 2 * cols),
        ],
        axis=0,
    )
    halo = passed_along(halo_in, "seq", 1)

    own_half = jnp.where(first, full_keys, full_values)
    seg_block = seg_rows(segment_ids, cols)
    payload = jnp.concatenate([own_half, seg_block], axis=0)
    halo, payload = lax.optimization_barrier((halo, payload))
    arrived = [passed_along(payload, "seq", d) for d in order]

    w_keys = jnp.concatenate([halo[:WINDOW, :cols], window_keys], axis=0)
    w_values = jnp.concatenate([halo[:WINDOW, cols:], window_values], axis=0)
    w_seg = jnp.concatenate([read_seg(halo[WINDOW:], WINDOW), segment_ids], axis=0)
    w_pos = seq_index * n - WINDOW + jnp.arange(n + WINDOW)
    w_bias = (query_pos, segment_ids, w_pos, w_seg, WINDOW)
    w_q = (window_query.reshape(n, -1) * 0.125).astype(jnp.bfloat16)
    w_do = window_grad_out.reshape(n, -1)
    g_split = groups // 2 if groups > 1 else groups
    w_out1 = attn_bwd(window_sinks, w_q, w_do, w_keys, w_values, w_bias, 0, g_split)

    w_out1, arrived = lax.optimization_barrier((w_out1, arrived))
    mine = jnp.concatenate(arrived, axis=0)
    other = lax.ppermute(mine, "rep", swap)
    step = n + seg_block.shape[0]
    key_parts, value_parts, seg_parts = [], [], []
    for idx in range(len(order)):
        a = mine[idx * step:(idx + 1) * step]
        b = other[idx * step:(idx + 1) * step]
        key_parts.append(jnp.where(first, a[:n], b[:n]))
        value_parts.append(jnp.where(first, b[:n], a[:n]))
        seg_parts.append(read_seg(a[n:], n))
    f_keys = jnp.concatenate(key_parts + [full_keys], axis=0)
    f_values = jnp.concatenate(value_parts + [full_values], axis=0)
    f_seg = jnp.concatenate(seg_parts + [segment_ids], axis=0)
    f_pos = (seq_index - (seq_count - 1)) * n + jnp.arange(seq_count * n)
    f_bias = (query_pos, segment_ids, f_pos, f_seg, None)
    f_q = (full_query.reshape(n, -1) * 0.125).astype(jnp.bfloat16)
    f_do = full_grad_out.reshape(n, -1)
    f_dq, f_dk, f_dv = attn_bwd(full_sinks, f_q, f_do, f_keys, f_values, f_bias, 0, groups)

    give = jnp.where(first, f_dv, f_dk)
    keep = jnp.where(first, f_dk, f_dv)
    summed = keep + lax.ppermute(give, "rep", swap)
    if g_split < groups:
        w_out2 = attn_bwd(window_sinks, w_q, w_do, w_keys, w_values, w_bias, g_split, groups - g_split)
        w_dq = jnp.concatenate([w_out1[0], w_out2[0]], axis=1)
        w_dk = jnp.concatenate([w_out1[1], w_out2[1]], axis=1)
        w_dv = jnp.concatenate([w_out1[2], w_out2[2]], axis=1)
    else:
        w_dq, w_dk, w_dv = w_out1

    f_final = summed[(seq_count - 1) * n:]
    back_w = jnp.zeros((WINDOW, 2 * cols), jnp.float32)
    for jj, d in enumerate(order):
        piece = summed[jj * n:(jj + 1) * n]
        if d == 1:
            piece = jnp.concatenate([piece, w_dk[:WINDOW], w_dv[:WINDOW]], axis=0)
        got = passed_along(piece.astype(jnp.bfloat16), "seq", -d).astype(jnp.float32)
        if d == 1:
            back_w = jnp.concatenate([got[n:n + WINDOW], got[n + WINDOW:]], axis=1)
            got = got[:n]
        f_final = f_final + got
    w_kv = jnp.concatenate([w_dk[WINDOW:], w_dv[WINDOW:]], axis=1)
    w_kv = jnp.concatenate([w_kv[: n - WINDOW], w_kv[n - WINDOW:] + back_w], axis=0)

    both = jnp.concatenate([w_kv, f_final], axis=1)
    peer = lax.ppermute(both, "rep", swap)
    w_sum = (w_kv + peer[:, :2 * cols]).astype(jnp.bfloat16)
    f_other = peer[:, 2 * cols:]
    f_dk_out = jnp.where(first, f_final, f_other).astype(jnp.bfloat16)
    f_dv_out = jnp.where(first, f_other, f_final).astype(jnp.bfloat16)
    return (
        w_dq.reshape(window_query.shape),
        w_sum[:, :cols],
        w_sum[:, cols:],
        f_dq.reshape(full_query.shape),
        f_dk_out,
        f_dv_out,
    )


def solution(mesh):
    placed = (
        P(("groups", "seq")),
        P(("groups", "seq"), "head", "rep"),
        P(("groups", "seq"), "head"),
        P(("groups", "seq"), "head"),
        P(("groups", "seq"), "head", "rep"),
        P("head", "rep"),
        P(("groups", "seq"), "head", "rep"),
        P(("groups", "seq"), "head"),
        P(("groups", "seq"), "head"),
        P(("groups", "seq"), "head", "rep"),
        P("head", "rep"),
    )
    return jax.shard_map(
        body,
        mesh=mesh,
        in_specs=placed,
        out_specs=(
            P(("groups", "seq"), "head", "rep"),
            P(("groups", "seq"), "head"),
            P(("groups", "seq"), "head"),
            P(("groups", "seq"), "head", "rep"),
            P(("groups", "seq"), "head"),
            P(("groups", "seq"), "head"),
        ),
        check_vma=False,
    )
```

```python
import functools
import math

import jax
import jax.numpy as jnp
from jax import lax
from jax.experimental import pallas as pl
from jax.experimental.pallas import tpu as pltpu
from jax.sharding import PartitionSpec as P

HD = 64
WINDOW = 128
NEG = -1e30
NT_DIMS = (((1,), (1,)), ((), ()))


def passed_along(value, axis, steps):
    count = lax.axis_size(axis)
    first, last = (max(0, -steps), min(count, count - steps))
    return lax.ppermute(value, axis, [(source, source + steps) for source in range(first, last)])


def pick_half(block, half):
    return jnp.where(half == 0, block[:, :HD], block[:, HD:])


def attn_bwd_kernel(g0, gn, pair, sink_ref, q_ref, do_ref, k_ref, v_ref, bias_ref, dq_ref, dk_ref, dv_ref):
    t = pl.program_id(0)
    i = pl.program_id(1)
    heads = q_ref.shape[1] // (HD * pair)

    @pl.when((t == 0) & (i == 0))
    def _():
        dk_ref[...] = jnp.zeros_like(dk_ref)
        dv_ref[...] = jnp.zeros_like(dv_ref)

    bias = bias_ref[...]
    k_block = k_ref[...]
    v_block = v_ref[...]
    dq_parts = []
    dk_parts = []
    dv_parts = []
    for h in range(pair):
        g = g0 + t * pair + h
        if pair >= 2:
            k = k_block[:, h * HD:(h + 1) * HD]
            v = v_block[:, h * HD:(h + 1) * HD]
        else:
            k = pick_half(k_block, g % 2)
            v = pick_half(v_block, g % 2)
        dk_acc = None
        dv_acc = None
        for j in range(heads):
            col = (h * heads + j) * HD
            q = q_ref[:, col:col + HD]
            do = do_ref[:, col:col + HD]
            sink = sink_ref[g, j]
            s = lax.dot_general(q, k, NT_DIMS, preferred_element_type=jnp.float32) + bias
            row_max = jnp.maximum(jnp.max(s, axis=1, keepdims=True), sink)
            e = jnp.exp(s - row_max)
            total = jnp.sum(e, axis=1, keepdims=True) + jnp.exp(sink - row_max)
            p = e * (1.0 / total)
            p_low = p.astype(jnp.bfloat16)
            dp = lax.dot_general(do, v, NT_DIMS, preferred_element_type=jnp.float32)
            delta = jnp.sum(p_low.astype(jnp.float32) * dp, axis=1, keepdims=True)
            ds_low = (p * (dp - delta)).astype(jnp.bfloat16)
            dq_parts.append(
                (jnp.dot(ds_low, k, preferred_element_type=jnp.float32) * 0.125).astype(dq_ref.dtype)
            )
            dk = jnp.dot(ds_low.T, q, preferred_element_type=jnp.float32)
            dv = jnp.dot(p_low.T, do, preferred_element_type=jnp.float32)
            dk_acc = dk if dk_acc is None else dk_acc + dk
            dv_acc = dv if dv_acc is None else dv_acc + dv
        dk_parts.append(dk_acc)
        dv_parts.append(dv_acc)
    dq_ref[...] = jnp.concatenate(dq_parts, axis=1)
    dk_step = jnp.concatenate(dk_parts, axis=1) if pair >= 2 else dk_parts[0]
    dv_step = jnp.concatenate(dv_parts, axis=1) if pair >= 2 else dv_parts[0]
    wide = pair * HD

    for tt in range(gn // pair):
        @pl.when(t == tt)
        def _():
            dk_ref[:, tt * wide:(tt + 1) * wide] += dk_step
            dv_ref[:, tt * wide:(tt + 1) * wide] += dv_step


def attn_bwd(sinks, queries, grads, keys, values, bias, g0, gn):
    n = queries.shape[0]
    m = keys.shape[0]
    heads = sinks.shape[1]
    if gn % 2 == 0 and g0 % gn == 0:
        pair = gn
    elif gn % 2 == 0 and g0 % 2 == 0:
        pair = 2
    else:
        pair = 1
    rows = n
    while rows > 8 and rows * m > (1 << 18):
        rows //= 2
    grid = (gn // pair, n // rows)
    width = heads * HD * pair
    if pair >= 2:
        key_width = pair * HD
        key_map = lambda t, i: (0, g0 // pair + t)
    else:
        key_width = 2 * HD
        key_map = lambda t, i: (0, (g0 + t) // 2)

    return pl.pallas_call(
        functools.partial(attn_bwd_kernel, g0, gn, pair),
        grid=grid,
        in_specs=[
            pl.BlockSpec(memory_space=pltpu.SMEM),
            pl.BlockSpec((rows, width), lambda t, i: (i, g0 // pair + t)),
            pl.BlockSpec((rows, width), lambda t, i: (i, g0 // pair + t)),
            pl.BlockSpec((m, key_width), key_map),
            pl.BlockSpec((m, key_width), key_map),
            pl.BlockSpec((rows, m), lambda t, i: (i, 0)),
        ],
        out_specs=[
            pl.BlockSpec((rows, width), lambda t, i: (i, t)),
            pl.BlockSpec((m, gn * HD), lambda t, i: (0, 0)),
            pl.BlockSpec((m, gn * HD), lambda t, i: (0, 0)),
        ],
        out_shape=[
            jax.ShapeDtypeStruct((n, gn * heads * HD), jnp.bfloat16),
            jax.ShapeDtypeStruct((m, gn * HD), jnp.float32),
            jax.ShapeDtypeStruct((m, gn * HD), jnp.float32),
        ],
        compiler_params=pltpu.CompilerParams(
            dimension_semantics=("arbitrary", "arbitrary"),
            vmem_limit_bytes=60 * 1024 * 1024,
        ),
        cost_estimate=pl.CostEstimate(
            flops=10 * gn * heads * n * m * HD,
            transcendentals=gn * heads * n * m,
            bytes_accessed=4 * n * m + 4 * n * gn * heads * HD * 3 + 12 * m * gn * HD,
        ),
    )(sinks, queries, grads, keys, values, bias)


def make_bias(query_pos, query_seg, key_pos, key_seg, window):
    distance = query_pos[:, None] - key_pos[None, :]
    visible = (distance >= 0) & (key_pos[None, :] >= 0) & (query_seg[:, None] == key_seg[None, :])
    if window is not None:
        visible = visible & (distance < window)
    return jnp.where(visible, 0.0, NEG).astype(jnp.float32)


def seg_rows(ids, width):
    count = ids.shape[0]
    lines = -(-count // width)
    flat = jnp.zeros((16 * (-(-lines // 16)) * width,), jnp.bfloat16)
    flat = flat.at[:count].set(ids.astype(jnp.bfloat16))
    return flat.reshape(-1, width)


def read_seg(block, count):
    return block.reshape(-1)[:count].astype(jnp.float32).astype(jnp.int32)


def body(
    segment_ids,
    window_query,
    window_keys,
    window_values,
    window_grad_out,
    window_sinks,
    full_query,
    full_keys,
    full_values,
    full_grad_out,
    full_sinks,
):
    n = window_query.shape[0]
    cols = window_keys.shape[1]
    groups = cols // HD
    seq_count = lax.axis_size("seq")
    seq_index = lax.axis_index("seq")
    rep_index = lax.axis_index("rep")
    first = rep_index == 0
    query_pos = seq_index * n + jnp.arange(n)
    order = list(range(seq_count - 1, 0, -1))
    swap = [(0, 1), (1, 0)]

    halo_in = jnp.concatenate(
        [
            jnp.concatenate([window_keys[n - WINDOW:], window_values[n - WINDOW:]], axis=1),
            seg_rows(segment_ids[n - WINDOW:], 2 * cols),
        ],
        axis=0,
    )
    halo = passed_along(halo_in, "seq", 1)

    own_half = jnp.where(first, full_keys, full_values)
    seg_block = seg_rows(segment_ids, cols)
    payload = jnp.concatenate([own_half, seg_block], axis=0)
    halo, payload = lax.optimization_barrier((halo, payload))
    arrived = [passed_along(payload, "seq", d) for d in order]

    w_keys = jnp.concatenate([halo[:WINDOW, :cols], window_keys], axis=0)
    w_values = jnp.concatenate([halo[:WINDOW, cols:], window_values], axis=0)
    w_seg = jnp.concatenate([read_seg(halo[WINDOW:], WINDOW), segment_ids], axis=0)
    w_pos = seq_index * n - WINDOW + jnp.arange(n + WINDOW)
    w_bias = make_bias(query_pos, segment_ids, w_pos, w_seg, WINDOW)
    w_q = (window_query.reshape(n, -1) * 0.125).astype(jnp.bfloat16)
    w_do = window_grad_out.reshape(n, -1)
    g_split = groups // 2 if groups > 1 else groups
    w_out1 = attn_bwd(window_sinks, w_q, w_do, w_keys, w_values, w_bias, 0, g_split)

    w_out1, arrived = lax.optimization_barrier((w_out1, arrived))
    mine = jnp.concatenate(arrived, axis=0)
    other = lax.ppermute(mine, "rep", swap)
    step = n + seg_block.shape[0]
    key_parts, value_parts, seg_parts = [], [], []
    for idx in range(len(order)):
        a = mine[idx * step:(idx + 1) * step]
        b = other[idx * step:(idx + 1) * step]
        key_parts.append(jnp.where(first, a[:n], b[:n]))
        value_parts.append(jnp.where(first, b[:n], a[:n]))
        seg_parts.append(read_seg(a[n:], n))
    f_keys = jnp.concatenate(key_parts + [full_keys], axis=0)
    f_values = jnp.concatenate(value_parts + [full_values], axis=0)
    f_seg = jnp.concatenate(seg_parts + [segment_ids], axis=0)
    f_pos = (seq_index - (seq_count - 1)) * n + jnp.arange(seq_count * n)
    f_bias = make_bias(query_pos, segment_ids, f_pos, f_seg, None)
    f_q = (full_query.reshape(n, -1) * 0.125).astype(jnp.bfloat16)
    f_do = full_grad_out.reshape(n, -1)
    f_dq, f_dk, f_dv = attn_bwd(full_sinks, f_q, f_do, f_keys, f_values, f_bias, 0, groups)

    to_second = lax.ppermute(f_dv, "rep", [(0, 1)])
    to_first = lax.ppermute(f_dk, "rep", [(1, 0)])
    summed = jnp.where(first, f_dk + to_first, f_dv + to_second)
    if g_split < groups:
        w_out2 = attn_bwd(window_sinks, w_q, w_do, w_keys, w_values, w_bias, g_split, groups - g_split)
        w_dq = jnp.concatenate([w_out1[0], w_out2[0]], axis=1)
        w_dk = jnp.concatenate([w_out1[1], w_out2[1]], axis=1)
        w_dv = jnp.concatenate([w_out1[2], w_out2[2]], axis=1)
    else:
        w_dq, w_dk, w_dv = w_out1

    f_final = summed[(seq_count - 1) * n:]
    back_w = jnp.zeros((WINDOW, 2 * cols), jnp.float32)
    for jj, d in enumerate(order):
        piece = summed[jj * n:(jj + 1) * n]
        if d == 1:
            piece = jnp.concatenate([piece, w_dk[:WINDOW], w_dv[:WINDOW]], axis=0)
        got = passed_along(piece.astype(jnp.bfloat16), "seq", -d).astype(jnp.float32)
        if d == 1:
            back_w = jnp.concatenate([got[n:n + WINDOW], got[n + WINDOW:]], axis=1)
            got = got[:n]
        f_final = f_final + got
    w_kv = jnp.concatenate([w_dk[WINDOW:], w_dv[WINDOW:]], axis=1)
    w_kv = jnp.concatenate([w_kv[: n - WINDOW], w_kv[n - WINDOW:] + back_w], axis=0)

    both = jnp.concatenate([w_kv, f_final], axis=1)
    peer = lax.ppermute(both, "rep", swap)
    w_sum = (w_kv + peer[:, :2 * cols]).astype(jnp.bfloat16)
    f_other = peer[:, 2 * cols:]
    f_dk_out = jnp.where(first, f_final, f_other).astype(jnp.bfloat16)
    f_dv_out = jnp.where(first, f_other, f_final).astype(jnp.bfloat16)
    return (
        w_dq.reshape(window_query.shape),
        w_sum[:, :cols],
        w_sum[:, cols:],
        f_dq.reshape(full_query.shape),
        f_dk_out,
        f_dv_out,
    )


def solution(mesh):
    placed = (
        P(("groups", "seq")),
        P(("groups", "seq"), "head", "rep"),
        P(("groups", "seq"), "head"),
        P(("groups", "seq"), "head"),
        P(("groups", "seq"), "head", "rep"),
        P("head", "rep"),
        P(("groups", "seq"), "head", "rep"),
        P(("groups", "seq"), "head"),
        P(("groups", "seq"), "head"),
        P(("groups", "seq"), "head", "rep"),
        P("head", "rep"),
    )
    return jax.shard_map(
        body,
        mesh=mesh,
        in_specs=placed,
        out_specs=(
            P(("groups", "seq"), "head", "rep"),
            P(("groups", "seq"), "head"),
            P(("groups", "seq"), "head"),
            P(("groups", "seq"), "head", "rep"),
            P(("groups", "seq"), "head"),
            P(("groups", "seq"), "head"),
        ),
        check_vma=False,
    )
```

```python
import functools
import math

import jax
import jax.numpy as jnp
from jax import lax
from jax.experimental import pallas as pl
from jax.experimental.pallas import tpu as pltpu
from jax.sharding import PartitionSpec as P

HD = 64
WINDOW = 128
NEG = -1e30
NT_DIMS = (((1,), (1,)), ((), ()))


def passed_along(value, axis, steps):
    count = lax.axis_size(axis)
    first, last = (max(0, -steps), min(count, count - steps))
    return lax.ppermute(value, axis, [(source, source + steps) for source in range(first, last)])


def pick_half(block, half):
    return jnp.where(half == 0, block[:, :HD], block[:, HD:])


def attn_bwd_kernel(g0, gn, pair, sink_ref, q_ref, do_ref, k_ref, v_ref, bias_ref, dq_ref, dk_ref, dv_ref):
    t = pl.program_id(0)
    i = pl.program_id(1)
    heads = q_ref.shape[1] // (HD * pair)

    @pl.when((t == 0) & (i == 0))
    def _():
        dk_ref[...] = jnp.zeros_like(dk_ref)
        dv_ref[...] = jnp.zeros_like(dv_ref)

    bias = bias_ref[...].astype(jnp.float32)
    k_block = k_ref[...]
    v_block = v_ref[...]
    dq_parts = []
    dk_parts = []
    dv_parts = []
    for h in range(pair):
        g = g0 + t * pair + h
        if pair >= 2:
            k = k_block[:, h * HD:(h + 1) * HD]
            v = v_block[:, h * HD:(h + 1) * HD]
        else:
            k = pick_half(k_block, g % 2)
            v = pick_half(v_block, g % 2)
        dk_acc = None
        dv_acc = None
        for j in range(heads):
            col = (h * heads + j) * HD
            q = q_ref[:, col:col + HD]
            do = do_ref[:, col:col + HD]
            sink = sink_ref[g, j]
            s = lax.dot_general(q, k, NT_DIMS, preferred_element_type=jnp.float32) + bias
            row_max = jnp.maximum(jnp.max(s, axis=1, keepdims=True), sink)
            e = jnp.exp(s - row_max)
            total = jnp.sum(e, axis=1, keepdims=True) + jnp.exp(sink - row_max)
            p = e * (1.0 / total)
            p_low = p.astype(jnp.bfloat16)
            dp = lax.dot_general(do, v, NT_DIMS, preferred_element_type=jnp.float32)
            delta = jnp.sum(p_low.astype(jnp.float32) * dp, axis=1, keepdims=True)
            ds_low = (p * (dp - delta)).astype(jnp.bfloat16)
            dq_parts.append(
                (jnp.dot(ds_low, k, preferred_element_type=jnp.float32) * 0.125).astype(dq_ref.dtype)
            )
            dk = jnp.dot(ds_low.T, q, preferred_element_type=jnp.float32)
            dv = jnp.dot(p_low.T, do, preferred_element_type=jnp.float32)
            dk_acc = dk if dk_acc is None else dk_acc + dk
            dv_acc = dv if dv_acc is None else dv_acc + dv
        dk_parts.append(dk_acc)
        dv_parts.append(dv_acc)
    dq_ref[...] = jnp.concatenate(dq_parts, axis=1)
    dk_step = jnp.concatenate(dk_parts, axis=1) if pair >= 2 else dk_parts[0]
    dv_step = jnp.concatenate(dv_parts, axis=1) if pair >= 2 else dv_parts[0]
    wide = pair * HD

    for tt in range(gn // pair):
        @pl.when(t == tt)
        def _():
            dk_ref[:, tt * wide:(tt + 1) * wide] += dk_step
            dv_ref[:, tt * wide:(tt + 1) * wide] += dv_step


def attn_bwd(sinks, queries, grads, keys, values, bias, g0, gn):
    n = queries.shape[0]
    m = keys.shape[0]
    heads = sinks.shape[1]
    if gn % 2 == 0 and g0 % gn == 0:
        pair = gn
    elif gn % 2 == 0 and g0 % 2 == 0:
        pair = 2
    else:
        pair = 1
    rows = n
    while rows > 8 and rows * m > (1 << 18):
        rows //= 2
    grid = (gn // pair, n // rows)
    width = heads * HD * pair
    if pair >= 2:
        key_width = pair * HD
        key_map = lambda t, i: (0, g0 // pair + t)
    else:
        key_width = 2 * HD
        key_map = lambda t, i: (0, (g0 + t) // 2)

    return pl.pallas_call(
        functools.partial(attn_bwd_kernel, g0, gn, pair),
        grid=grid,
        in_specs=[
            pl.BlockSpec(memory_space=pltpu.SMEM),
            pl.BlockSpec((rows, width), lambda t, i: (i, g0 // pair + t)),
            pl.BlockSpec((rows, width), lambda t, i: (i, g0 // pair + t)),
            pl.BlockSpec((m, key_width), key_map),
            pl.BlockSpec((m, key_width), key_map),
            pl.BlockSpec((rows, m), lambda t, i: (i, 0)),
        ],
        out_specs=[
            pl.BlockSpec((rows, width), lambda t, i: (i, t)),
            pl.BlockSpec((m, gn * HD), lambda t, i: (0, 0)),
            pl.BlockSpec((m, gn * HD), lambda t, i: (0, 0)),
        ],
        out_shape=[
            jax.ShapeDtypeStruct((n, gn * heads * HD), jnp.bfloat16),
            jax.ShapeDtypeStruct((m, gn * HD), jnp.float32),
            jax.ShapeDtypeStruct((m, gn * HD), jnp.float32),
        ],
        compiler_params=pltpu.CompilerParams(
            dimension_semantics=("arbitrary", "arbitrary"),
            vmem_limit_bytes=60 * 1024 * 1024,
        ),
        cost_estimate=pl.CostEstimate(
            flops=10 * gn * heads * n * m * HD,
            transcendentals=gn * heads * n * m,
            bytes_accessed=2 * n * m + 4 * n * gn * heads * HD * 3 + 12 * m * gn * HD,
        ),
    )(sinks, queries, grads, keys, values, bias)


def make_bias(query_pos, query_seg, key_pos, key_seg, window):
    distance = query_pos[:, None] - key_pos[None, :]
    visible = (distance >= 0) & (key_pos[None, :] >= 0) & (query_seg[:, None] == key_seg[None, :])
    if window is not None:
        visible = visible & (distance < window)
    return jnp.where(visible, 0.0, NEG).astype(jnp.bfloat16)


def seg_rows(ids, width):
    count = ids.shape[0]
    lines = -(-count // width)
    flat = jnp.zeros((16 * (-(-lines // 16)) * width,), jnp.bfloat16)
    flat = flat.at[:count].set(ids.astype(jnp.bfloat16))
    return flat.reshape(-1, width)


def read_seg(block, count):
    return block.reshape(-1)[:count].astype(jnp.float32).astype(jnp.int32)


def body(
    segment_ids,
    window_query,
    window_keys,
    window_values,
    window_grad_out,
    window_sinks,
    full_query,
    full_keys,
    full_values,
    full_grad_out,
    full_sinks,
):
    n = window_query.shape[0]
    cols = window_keys.shape[1]
    groups = cols // HD
    seq_count = lax.axis_size("seq")
    seq_index = lax.axis_index("seq")
    rep_index = lax.axis_index("rep")
    first = rep_index == 0
    query_pos = seq_index * n + jnp.arange(n)
    order = list(range(seq_count - 1, 0, -1))
    swap = [(0, 1), (1, 0)]

    halo_in = jnp.concatenate(
        [
            jnp.concatenate([window_keys[n - WINDOW:], window_values[n - WINDOW:]], axis=1),
            seg_rows(segment_ids[n - WINDOW:], 2 * cols),
        ],
        axis=0,
    )
    halo = passed_along(halo_in, "seq", 1)

    own_half = jnp.where(first, full_keys, full_values)
    seg_block = seg_rows(segment_ids, cols)
    payload = jnp.concatenate([own_half, seg_block], axis=0)
    halo, payload = lax.optimization_barrier((halo, payload))
    arrived = [passed_along(payload, "seq", d) for d in order]

    w_keys = jnp.concatenate([halo[:WINDOW, :cols], window_keys], axis=0)
    w_values = jnp.concatenate([halo[:WINDOW, cols:], window_values], axis=0)
    w_seg = jnp.concatenate([read_seg(halo[WINDOW:], WINDOW), segment_ids], axis=0)
    w_pos = seq_index * n - WINDOW + jnp.arange(n + WINDOW)
    w_bias = make_bias(query_pos, segment_ids, w_pos, w_seg, WINDOW)
    w_q = (window_query.reshape(n, -1) * 0.125).astype(jnp.bfloat16)
    w_do = window_grad_out.reshape(n, -1)
    g_split = groups // 2 if groups > 1 else groups
    w_out1 = attn_bwd(window_sinks, w_q, w_do, w_keys, w_values, w_bias, 0, g_split)

    w_out1, arrived = lax.optimization_barrier((w_out1, arrived))
    mine = jnp.concatenate(arrived, axis=0)
    other = lax.ppermute(mine, "rep", swap)
    step = n + seg_block.shape[0]
    key_parts, value_parts, seg_parts = [], [], []
    for idx in range(len(order)):
        a = mine[idx * step:(idx + 1) * step]
        b = other[idx * step:(idx + 1) * step]
        key_parts.append(jnp.where(first, a[:n], b[:n]))
        value_parts.append(jnp.where(first, b[:n], a[:n]))
        seg_parts.append(read_seg(a[n:], n))
    f_keys = jnp.concatenate(key_parts + [full_keys], axis=0)
    f_values = jnp.concatenate(value_parts + [full_values], axis=0)
    f_seg = jnp.concatenate(seg_parts + [segment_ids], axis=0)
    f_pos = (seq_index - (seq_count - 1)) * n + jnp.arange(seq_count * n)
    f_bias = make_bias(query_pos, segment_ids, f_pos, f_seg, None)
    f_q = (full_query.reshape(n, -1) * 0.125).astype(jnp.bfloat16)
    f_do = full_grad_out.reshape(n, -1)
    f_dq, f_dk, f_dv = attn_bwd(full_sinks, f_q, f_do, f_keys, f_values, f_bias, 0, groups)

    give = jnp.where(first, f_dv, f_dk)
    keep = jnp.where(first, f_dk, f_dv)
    summed = keep + lax.ppermute(give, "rep", swap)
    if g_split < groups:
        w_out2 = attn_bwd(window_sinks, w_q, w_do, w_keys, w_values, w_bias, g_split, groups - g_split)
        w_dq = jnp.concatenate([w_out1[0], w_out2[0]], axis=1)
        w_dk = jnp.concatenate([w_out1[1], w_out2[1]], axis=1)
        w_dv = jnp.concatenate([w_out1[2], w_out2[2]], axis=1)
    else:
        w_dq, w_dk, w_dv = w_out1

    f_final = summed[(seq_count - 1) * n:]
    back_w = jnp.zeros((WINDOW, 2 * cols), jnp.float32)
    for jj, d in enumerate(order):
        piece = summed[jj * n:(jj + 1) * n]
        if d == 1:
            piece = jnp.concatenate([piece, w_dk[:WINDOW], w_dv[:WINDOW]], axis=0)
        got = passed_along(piece.astype(jnp.bfloat16), "seq", -d).astype(jnp.float32)
        if d == 1:
            back_w = jnp.concatenate([got[n:n + WINDOW], got[n + WINDOW:]], axis=1)
            got = got[:n]
        f_final = f_final + got
    w_kv = jnp.concatenate([w_dk[WINDOW:], w_dv[WINDOW:]], axis=1)
    w_kv = jnp.concatenate([w_kv[: n - WINDOW], w_kv[n - WINDOW:] + back_w], axis=0)

    both = jnp.concatenate([w_kv, f_final], axis=1)
    peer = lax.ppermute(both, "rep", swap)
    w_sum = (w_kv + peer[:, :2 * cols]).astype(jnp.bfloat16)
    f_other = peer[:, 2 * cols:]
    f_dk_out = jnp.where(first, f_final, f_other).astype(jnp.bfloat16)
    f_dv_out = jnp.where(first, f_other, f_final).astype(jnp.bfloat16)
    return (
        w_dq.reshape(window_query.shape),
        w_sum[:, :cols],
        w_sum[:, cols:],
        f_dq.reshape(full_query.shape),
        f_dk_out,
        f_dv_out,
    )


def solution(mesh):
    placed = (
        P(("groups", "seq")),
        P(("groups", "seq"), "head", "rep"),
        P(("groups", "seq"), "head"),
        P(("groups", "seq"), "head"),
        P(("groups", "seq"), "head", "rep"),
        P("head", "rep"),
        P(("groups", "seq"), "head", "rep"),
        P(("groups", "seq"), "head"),
        P(("groups", "seq"), "head"),
        P(("groups", "seq"), "head", "rep"),
        P("head", "rep"),
    )
    return jax.shard_map(
        body,
        mesh=mesh,
        in_specs=placed,
        out_specs=(
            P(("groups", "seq"), "head", "rep"),
            P(("groups", "seq"), "head"),
            P(("groups", "seq"), "head"),
            P(("groups", "seq"), "head", "rep"),
            P(("groups", "seq"), "head"),
            P(("groups", "seq"), "head"),
        ),
        check_vma=False,
    )
```

```python
import functools
import math

import jax
import jax.numpy as jnp
from jax import lax
from jax.experimental import pallas as pl
from jax.experimental.pallas import tpu as pltpu
from jax.sharding import PartitionSpec as P

HD = 64
WINDOW = 128
NEG = -1e30
NT_DIMS = (((1,), (1,)), ((), ()))


def passed_along(value, axis, steps):
    count = lax.axis_size(axis)
    first, last = (max(0, -steps), min(count, count - steps))
    return lax.ppermute(value, axis, [(source, source + steps) for source in range(first, last)])


def pick_half(block, half):
    return jnp.where(half == 0, block[:, :HD], block[:, HD:])


def attn_bwd_kernel(g0, gn, pair, single, sink_ref, q_ref, do_ref, k_ref, v_ref, bias_ref, dq_ref, dk_ref, dv_ref):
    t = pl.program_id(0)
    i = pl.program_id(1)
    heads = q_ref.shape[1] // (HD * pair)

    if not single:
        @pl.when((t == 0) & (i == 0))
        def _():
            dk_ref[...] = jnp.zeros_like(dk_ref)
            dv_ref[...] = jnp.zeros_like(dv_ref)

    bias = bias_ref[...].astype(jnp.float32)
    k_block = k_ref[...]
    v_block = v_ref[...]
    dq_parts = []
    dk_parts = []
    dv_parts = []
    for h in range(pair):
        g = g0 + t * pair + h
        if pair >= 2:
            k = k_block[:, h * HD:(h + 1) * HD]
            v = v_block[:, h * HD:(h + 1) * HD]
        else:
            k = pick_half(k_block, g % 2)
            v = pick_half(v_block, g % 2)
        dk_acc = None
        dv_acc = None
        for j in range(heads):
            col = (h * heads + j) * HD
            q = q_ref[:, col:col + HD]
            do = do_ref[:, col:col + HD]
            sink = sink_ref[g, j]
            s = lax.dot_general(q, k, NT_DIMS, preferred_element_type=jnp.float32) + bias
            row_max = jnp.maximum(jnp.max(s, axis=1, keepdims=True), sink)
            e = jnp.exp(s - row_max)
            total = jnp.sum(e, axis=1, keepdims=True) + jnp.exp(sink - row_max)
            p = e * (1.0 / total)
            p_low = p.astype(jnp.bfloat16)
            dp = lax.dot_general(do, v, NT_DIMS, preferred_element_type=jnp.float32)
            delta = jnp.sum(p_low.astype(jnp.float32) * dp, axis=1, keepdims=True)
            ds_low = (p * (dp - delta)).astype(jnp.bfloat16)
            dq_parts.append(
                (jnp.dot(ds_low, k, preferred_element_type=jnp.float32) * 0.125).astype(dq_ref.dtype)
            )
            dk = jnp.dot(ds_low.T, q, preferred_element_type=jnp.float32)
            dv = jnp.dot(p_low.T, do, preferred_element_type=jnp.float32)
            dk_acc = dk if dk_acc is None else dk_acc + dk
            dv_acc = dv if dv_acc is None else dv_acc + dv
        dk_parts.append(dk_acc)
        dv_parts.append(dv_acc)
    dq_ref[...] = jnp.concatenate(dq_parts, axis=1)
    dk_step = jnp.concatenate(dk_parts, axis=1) if pair >= 2 else dk_parts[0]
    dv_step = jnp.concatenate(dv_parts, axis=1) if pair >= 2 else dv_parts[0]
    wide = pair * HD

    if single:
        dk_ref[...] = dk_step
        dv_ref[...] = dv_step
        return
    for tt in range(gn // pair):
        @pl.when(t == tt)
        def _():
            dk_ref[:, tt * wide:(tt + 1) * wide] += dk_step
            dv_ref[:, tt * wide:(tt + 1) * wide] += dv_step


def attn_bwd(sinks, queries, grads, keys, values, bias, g0, gn):
    n = queries.shape[0]
    m = keys.shape[0]
    heads = sinks.shape[1]
    if gn % 2 == 0 and g0 % gn == 0:
        pair = gn
    elif gn % 2 == 0 and g0 % 2 == 0:
        pair = 2
    else:
        pair = 1
    rows = n
    while rows > 8 and rows * m > (1 << 18):
        rows //= 2
    grid = (gn // pair, n // rows)
    width = heads * HD * pair
    if pair >= 2:
        key_width = pair * HD
        key_map = lambda t, i: (0, g0 // pair + t)
    else:
        key_width = 2 * HD
        key_map = lambda t, i: (0, (g0 + t) // 2)

    return pl.pallas_call(
        functools.partial(attn_bwd_kernel, g0, gn, pair, gn == pair and rows == n),
        grid=grid,
        in_specs=[
            pl.BlockSpec(memory_space=pltpu.SMEM),
            pl.BlockSpec((rows, width), lambda t, i: (i, g0 // pair + t)),
            pl.BlockSpec((rows, width), lambda t, i: (i, g0 // pair + t)),
            pl.BlockSpec((m, key_width), key_map),
            pl.BlockSpec((m, key_width), key_map),
            pl.BlockSpec((rows, m), lambda t, i: (i, 0)),
        ],
        out_specs=[
            pl.BlockSpec((rows, width), lambda t, i: (i, t)),
            pl.BlockSpec((m, gn * HD), lambda t, i: (0, 0)),
            pl.BlockSpec((m, gn * HD), lambda t, i: (0, 0)),
        ],
        out_shape=[
            jax.ShapeDtypeStruct((n, gn * heads * HD), jnp.bfloat16),
            jax.ShapeDtypeStruct((m, gn * HD), jnp.float32),
            jax.ShapeDtypeStruct((m, gn * HD), jnp.float32),
        ],
        compiler_params=pltpu.CompilerParams(
            dimension_semantics=("arbitrary", "arbitrary"),
            vmem_limit_bytes=60 * 1024 * 1024,
        ),
        cost_estimate=pl.CostEstimate(
            flops=10 * gn * heads * n * m * HD,
            transcendentals=gn * heads * n * m,
            bytes_accessed=2 * n * m + 4 * n * gn * heads * HD * 3 + 12 * m * gn * HD,
        ),
    )(sinks, queries, grads, keys, values, bias)


def make_bias(query_pos, query_seg, key_pos, key_seg, window):
    distance = query_pos[:, None] - key_pos[None, :]
    visible = (distance >= 0) & (key_pos[None, :] >= 0) & (query_seg[:, None] == key_seg[None, :])
    if window is not None:
        visible = visible & (distance < window)
    return jnp.where(visible, 0.0, NEG).astype(jnp.bfloat16)


def seg_rows(ids, width):
    count = ids.shape[0]
    lines = -(-count // width)
    flat = jnp.zeros((16 * (-(-lines // 16)) * width,), jnp.bfloat16)
    flat = flat.at[:count].set(ids.astype(jnp.bfloat16))
    return flat.reshape(-1, width)


def read_seg(block, count):
    return block.reshape(-1)[:count].astype(jnp.float32).astype(jnp.int32)


def body(
    segment_ids,
    window_query,
    window_keys,
    window_values,
    window_grad_out,
    window_sinks,
    full_query,
    full_keys,
    full_values,
    full_grad_out,
    full_sinks,
):
    n = window_query.shape[0]
    cols = window_keys.shape[1]
    groups = cols // HD
    seq_count = lax.axis_size("seq")
    seq_index = lax.axis_index("seq")
    rep_index = lax.axis_index("rep")
    first = rep_index == 0
    query_pos = seq_index * n + jnp.arange(n)
    order = list(range(seq_count - 1, 0, -1))
    swap = [(0, 1), (1, 0)]

    halo_in = jnp.concatenate(
        [
            jnp.concatenate([window_keys[n - WINDOW:], window_values[n - WINDOW:]], axis=1),
            seg_rows(segment_ids[n - WINDOW:], 2 * cols),
        ],
        axis=0,
    )
    halo = passed_along(halo_in, "seq", 1)

    own_half = jnp.where(first, full_keys, full_values)
    seg_block = seg_rows(segment_ids, cols)
    payload = jnp.concatenate([own_half, seg_block], axis=0)
    halo, payload = lax.optimization_barrier((halo, payload))
    arrived = [passed_along(payload, "seq", d) for d in order]

    w_keys = jnp.concatenate([halo[:WINDOW, :cols], window_keys], axis=0)
    w_values = jnp.concatenate([halo[:WINDOW, cols:], window_values], axis=0)
    w_seg = jnp.concatenate([read_seg(halo[WINDOW:], WINDOW), segment_ids], axis=0)
    w_pos = seq_index * n - WINDOW + jnp.arange(n + WINDOW)
    w_bias = make_bias(query_pos, segment_ids, w_pos, w_seg, WINDOW)
    w_q = (window_query.reshape(n, -1) * 0.125).astype(jnp.bfloat16)
    w_do = window_grad_out.reshape(n, -1)
    g_split = groups // 2 if groups > 1 else groups
    w_out1 = attn_bwd(window_sinks, w_q, w_do, w_keys, w_values, w_bias, 0, g_split)

    w_out1, arrived = lax.optimization_barrier((w_out1, arrived))
    mine = jnp.concatenate(arrived, axis=0)
    other = lax.ppermute(mine, "rep", swap)
    step = n + seg_block.shape[0]
    key_parts, value_parts, seg_parts = [], [], []
    for idx in range(len(order)):
        a = mine[idx * step:(idx + 1) * step]
        b = other[idx * step:(idx + 1) * step]
        key_parts.append(jnp.where(first, a[:n], b[:n]))
        value_parts.append(jnp.where(first, b[:n], a[:n]))
        seg_parts.append(read_seg(a[n:], n))
    f_keys = jnp.concatenate(key_parts + [full_keys], axis=0)
    f_values = jnp.concatenate(value_parts + [full_values], axis=0)
    f_seg = jnp.concatenate(seg_parts + [segment_ids], axis=0)
    f_pos = (seq_index - (seq_count - 1)) * n + jnp.arange(seq_count * n)
    f_bias = make_bias(query_pos, segment_ids, f_pos, f_seg, None)
    f_q = (full_query.reshape(n, -1) * 0.125).astype(jnp.bfloat16)
    f_do = full_grad_out.reshape(n, -1)
    f_dq, f_dk, f_dv = attn_bwd(full_sinks, f_q, f_do, f_keys, f_values, f_bias, 0, groups)

    give = jnp.where(first, f_dv, f_dk)
    keep = jnp.where(first, f_dk, f_dv)
    summed = keep + lax.ppermute(give, "rep", swap)
    if g_split < groups:
        w_out2 = attn_bwd(window_sinks, w_q, w_do, w_keys, w_values, w_bias, g_split, groups - g_split)
        w_dq = jnp.concatenate([w_out1[0], w_out2[0]], axis=1)
        w_dk = jnp.concatenate([w_out1[1], w_out2[1]], axis=1)
        w_dv = jnp.concatenate([w_out1[2], w_out2[2]], axis=1)
    else:
        w_dq, w_dk, w_dv = w_out1

    f_final = summed[(seq_count - 1) * n:]
    back_w = jnp.zeros((WINDOW, 2 * cols), jnp.float32)
    for jj, d in enumerate(order):
        piece = summed[jj * n:(jj + 1) * n]
        if d == 1:
            piece = jnp.concatenate([piece, w_dk[:WINDOW], w_dv[:WINDOW]], axis=0)
        got = passed_along(piece.astype(jnp.bfloat16), "seq", -d).astype(jnp.float32)
        if d == 1:
            back_w = jnp.concatenate([got[n:n + WINDOW], got[n + WINDOW:]], axis=1)
            got = got[:n]
        f_final = f_final + got
    w_kv = jnp.concatenate([w_dk[WINDOW:], w_dv[WINDOW:]], axis=1)
    w_kv = jnp.concatenate([w_kv[: n - WINDOW], w_kv[n - WINDOW:] + back_w], axis=0)

    both = jnp.concatenate([w_kv, f_final], axis=1)
    peer = lax.ppermute(both, "rep", swap)
    w_sum = (w_kv + peer[:, :2 * cols]).astype(jnp.bfloat16)
    f_other = peer[:, 2 * cols:]
    f_dk_out = jnp.where(first, f_final, f_other).astype(jnp.bfloat16)
    f_dv_out = jnp.where(first, f_other, f_final).astype(jnp.bfloat16)
    return (
        w_dq.reshape(window_query.shape),
        w_sum[:, :cols],
        w_sum[:, cols:],
        f_dq.reshape(full_query.shape),
        f_dk_out,
        f_dv_out,
    )


def solution(mesh):
    placed = (
        P(("groups", "seq")),
        P(("groups", "seq"), "head", "rep"),
        P(("groups", "seq"), "head"),
        P(("groups", "seq"), "head"),
        P(("groups", "seq"), "head", "rep"),
        P("head", "rep"),
        P(("groups", "seq"), "head", "rep"),
        P(("groups", "seq"), "head"),
        P(("groups", "seq"), "head"),
        P(("groups", "seq"), "head", "rep"),
        P("head", "rep"),
    )
    return jax.shard_map(
        body,
        mesh=mesh,
        in_specs=placed,
        out_specs=(
            P(("groups", "seq"), "head", "rep"),
            P(("groups", "seq"), "head"),
            P(("groups", "seq"), "head"),
            P(("groups", "seq"), "head", "rep"),
            P(("groups", "seq"), "head"),
            P(("groups", "seq"), "head"),
        ),
        check_vma=False,
    )
```
